32 devices in a mesh: dom: 4 (over y, x), st: 8 (over z, core).
Axes of the slice: x: 2, y: 2, z: 4, core: 2. Of those that a mesh axis runs over, the one named last changes fastest.
Arguments:
- states: bfloat16 [6912, 1024], P('dom', 'st'), may hold values from -6 to 6
- inv_mass: float32 [6912], P('dom'), may hold values from 0.4 to 1
- potential: float32 [6912], P('dom'), may hold values from -1 to 0.5
- cell_matrix: bfloat16 [343, 343], replicated, may hold values from -0.21 to 2, as said below
- connect: int32 [32, 343], P('dom'), may hold values from 0 to 1871, as said below
- face_rows: int32 [576], P('dom'), may hold values from 0 to 1727, as said below
- rotation: bfloat16 [512, 1024], P(None, 'st'), may hold values from -0.25 to 0.25
Outputs:
- rotated: float32 [6912, 1024], P('dom', 'st')
The draws below stay inside these ranges and needn't reach their ends.
Inputs may be any that keep to these rules, and one draw needn't show every extreme that they name: Row c of a device's block of connect lists the nodes of one of its 8 cells, in the order of cell_matrix's rows; each number below 1728 appears somewhere in the block. `face_rows`: A device's block holds 144 different node rows of that device. `cell_matrix`: Symmetric.
All inputs are finite; a program needn't handle non-finite values.
Results may differ from the reference program's by a relative error of at most 0.0031.
Values may be sent and summed in bfloat16 or wider, within the bound.
No kernel may reach another device: no remote copies, remote signals or barrier semaphores. Data moves between devices by JAX's collectives and lax.ppermute only.
A program may use at most 64 MiB of HBM per device.

```python
import math
import jax
import jax.numpy as jnp
from jax import lax

DEG = 6
POLY = 3
CX = 2
CY = 2
CZ = 2
NPC = 343
CELLS = 8
NODES_DEV = 1728
PLANE = 144
NODES = 6912
CELLS_ALL = 32
STATES = 1024
BLOCK = 512


def cell_layout(key):
    dom_count = NODES // NODES_DEV
    span_second = DEG * CY
    span_third = DEG * CZ
    side = DEG + 1

    def one_device(device):
        device_key = jax.random.fold_in(key, device)
        labels = jax.random.permutation(jax.random.fold_in(device_key, 1), NODES_DEV).astype(jnp.int32)
        cell_order = jax.random.permutation(jax.random.fold_in(device_key, 2), CELLS).astype(jnp.int32)
        cell_first = cell_order // (CY * CZ)
        cell_second = cell_order // CZ % CY
        cell_third = cell_order % CZ
        corner = jnp.arange(NPC, dtype=jnp.int32)
        step_first = corner // (side * side)
        step_second = corner // side % side
        step_third = corner % side
        node_first = cell_first[:, None] * DEG + step_first[None, :]
        node_second = (cell_second[:, None] * DEG + step_second[None, :]) % span_second
        node_third = (cell_third[:, None] * DEG + step_third[None, :]) % span_third
        inside = node_first < DEG * CX
        canonical = (jnp.minimum(node_first, DEG * CX - 1) * span_second + node_second) * span_third + node_third
        rim_index = node_second * span_third + node_third
        numbers = jnp.where(inside, labels[canonical], NODES_DEV + rim_index).astype(jnp.int32)
        return (numbers, labels[:PLANE])
    return jax.vmap(one_device)(jnp.arange(dom_count, dtype=jnp.int32))


def draw_connect(key, part):
    numbers, face_lists = cell_layout(jax.random.fold_in(key, 7))
    return numbers.reshape(CELLS_ALL, NPC).astype(jnp.int32)


def draw_face_rows(key, part):
    numbers, face_lists = cell_layout(jax.random.fold_in(key, 7))
    return face_lists.reshape(-1).astype(jnp.int32)


def draw_cell_matrix(key, part):
    key_rough = jax.random.fold_in(key, 11)
    key_diag = jax.random.fold_in(key, 12)
    coupling_raw = jax.random.normal(key_rough, (NPC, NPC), jnp.float32)
    spread = 0.6 / math.sqrt(NPC)
    coupling = jnp.clip((coupling_raw + coupling_raw.T) * (0.70710678 * spread), -0.2, 0.2)
    diagonal = jnp.exp(jax.random.uniform(key_diag, (NPC,), jnp.float32, math.log(0.5), math.log(2.0)))
    identity = jnp.eye(NPC, dtype=jnp.float32)
    return (coupling * (1.0 - identity) + diagonal[:, None] * identity).astype(jnp.bfloat16)


def steps_of(rng, dims, split, least, high):
    def one(dim, parts):
        heights = jax.random.uniform(jax.random.fold_in(jax.random.fold_in(rng, 6), dim), (parts,), jnp.float32, least / len(split), high / len(split))
        return jnp.repeat(jnp.exp(heights), dims[dim] // parts).reshape((-1,) + (1,) * (len(dims) - dim - 1))

    loudness = one(*split[0])
    for cut in split[1:]:
        loudness = loudness * one(*cut)
    return loudness


def centred(key, dims, scale, most, split=(), kind=jnp.bfloat16):
    result = scale * jax.random.normal(key, dims, jnp.float32)
    if split:
        result = result * steps_of(key, dims, split, -0.22, 0.18)
    return jnp.clip(result, -most, most).astype(kind)


def setup_inputs(seed: int = 0) -> dict:
    key_of = jax.random.split(jax.random.key(seed), 8)
    states = centred(key_of[0], (NODES, STATES), 1.0, 6.0, ((0, 4), (1, 8)))
    inv_mass = jnp.clip(jnp.exp(math.log(1.0) - 0.9162907 * jax.random.uniform(key_of[1], (NODES,), jnp.float32) ** steps_of(key_of[1], (NODES,), ((0, 4),), -0.2, 0.2)), 0.4, 1.0)
    potential = jnp.clip(-1.0 + 1.5 * jax.random.uniform(key_of[2], (NODES,), jnp.float32) ** steps_of(key_of[2], (NODES,), ((0, 4),), -0.2, 0.2), -1.0, 0.5)
    cell_matrix = draw_cell_matrix(jax.random.fold_in(key_of[7], 71), 0)
    connect = draw_connect(jax.random.fold_in(key_of[7], 71), 0)
    face_rows = draw_face_rows(jax.random.fold_in(key_of[7], 71), 0)
    rotation = centred(key_of[6], (BLOCK, STATES), BLOCK ** -0.5, 0.25, ((1, 8),))
    return dict(states=states, inv_mass=inv_mass, potential=potential, cell_matrix=cell_matrix, connect=connect, face_rows=face_rows, rotation=rotation)


centre = 10.0
half_span = 10.0


def pick_rows(lookup, picked):
    return lookup[picked]


def global_cells(connect, face_rows):
    dom_count = NODES // NODES_DEV
    numbers = connect.reshape(dom_count, CELLS * NPC)
    face_lists = face_rows.reshape(dom_count, PLANE)
    following = jnp.roll(face_lists, -1, axis=0)
    starts = jnp.arange(dom_count, dtype=jnp.int32) * NODES_DEV
    rim_index = jnp.clip(numbers - NODES_DEV, 0, PLANE - 1)
    across = jax.vmap(pick_rows)(following, rim_index)
    own_rows = starts[:, None] + numbers
    beyond = jnp.roll(starts, -1)[:, None] + across
    return jnp.where(numbers < NODES_DEV, own_rows, beyond).reshape(-1).astype(jnp.int32)


def hamiltonian(field_in, node_rows, cell_matrix, inv_mass, potential):
    state_count = field_in.shape[1]
    scaled = inv_mass[:, None] * field_in
    values = lax.optimization_barrier(scaled[node_rows].astype(jnp.bfloat16)).astype(jnp.float32)
    values = values.reshape(CELLS_ALL, NPC, state_count)
    matrix = cell_matrix.astype(jnp.float32)
    products = jnp.einsum("ij,cjb->cib", matrix, values, precision=lax.Precision.HIGHEST)
    summed = jnp.zeros(field_in.shape, jnp.float32).at[node_rows].add(products.reshape(-1, state_count))
    return inv_mass[:, None] * summed + potential[:, None] * field_in


def reference(states, inv_mass, potential, cell_matrix, connect, face_rows, rotation):
    node_rows = global_cells(connect, face_rows)
    block_count = STATES // BLOCK
    blocks = states.astype(jnp.float32).reshape(NODES, block_count, BLOCK).transpose(1, 0, 2)
    turn_blocks = rotation.reshape(BLOCK, block_count, BLOCK).transpose(1, 0, 2)

    def scaled_step(field_in):
        return (hamiltonian(field_in, node_rows, cell_matrix, inv_mass, potential) - centre * field_in) / half_span

    def one_block(inputs):
        field_in, turn_block = inputs
        previous = field_in
        current = scaled_step(field_in)
        for repeat in range(POLY - 1):
            previous, current = current, 2.0 * scaled_step(current) - previous
        return jnp.dot(current.astype(jnp.bfloat16), turn_block, preferred_element_type=jnp.float32)

    rotated = lax.map(one_block, (blocks, turn_blocks))
    return rotated.transpose(1, 0, 2).reshape(NODES, STATES)
```

```python
import jax
import jax.numpy as jnp
from jax import lax
from jax.sharding import PartitionSpec as P

POLY = 3


centre = 10.0
half_span = 10.0


def ring(block, axis, step):
    count = lax.axis_size(axis)
    route = [(i, (i + step) % count) for i in range(count)]
    return lax.ppermute(block, axis, route)


def from_partner(block, axis, distance):
    count = lax.axis_size(axis)
    route = []
    for low in range(count):
        high = low | 1 << distance
        if high != low and high < count:
            route += [(low, high), (high, low)]
    return lax.ppermute(block, axis, route)


def split_dot(select, value):
    high = value.astype(jnp.bfloat16)
    low = (value - high.astype(jnp.float32)).astype(jnp.bfloat16)
    width = value.shape[1]
    both = jnp.dot(select, jnp.concatenate([high, low], 1), preferred_element_type=jnp.float32)
    return both[:, :width] + both[:, width:]


def body(states, inv_mass, potential, cell_matrix, connect, face_rows, rotation):
    node_count, state_count = states.shape
    cell_count, cell_size = connect.shape
    face_count = face_rows.shape[0]
    wide_count = node_count + face_count
    cell_rows = connect.reshape(-1)
    wide_ids = lax.broadcasted_iota(jnp.int32, (wide_count, 1), 0)
    gather_sel = (cell_rows[:, None] == wide_ids[:, 0][None, :]).astype(jnp.bfloat16)
    scatter_sel = (wide_ids == cell_rows[None, :]).astype(jnp.bfloat16)
    face_sel = (face_rows[:, None] == cell_rows[None, :]).astype(jnp.bfloat16)
    rim_sel = jnp.concatenate([face_sel, scatter_sel[node_count:]], 0)
    face_put = (wide_ids[:node_count] == face_rows[None, :]).astype(jnp.bfloat16)

    face_states = states[face_rows].astype(jnp.float32)
    ghost_states, ghost_mass, ghost_potential = ring(
        (face_states, inv_mass[face_rows], potential[face_rows]), "dom", -1
    )
    field_start = jnp.concatenate([states.astype(jnp.float32), ghost_states], 0)
    wide_mass = jnp.concatenate([inv_mass, ghost_mass], 0)
    wide_potential = jnp.concatenate([potential, ghost_potential], 0)

    def operate(field_in):
        weighted = (wide_mass[:, None] * field_in).astype(jnp.bfloat16)
        values = jnp.dot(gather_sel, weighted, preferred_element_type=jnp.float32)
        values = values.astype(jnp.bfloat16).reshape(cell_count, cell_size, state_count)
        products = jnp.einsum(
            "ij,cjb->cib", cell_matrix, values, preferred_element_type=jnp.float32
        ).reshape(-1, state_count)
        high = products.astype(jnp.bfloat16)
        low = (products - high.astype(jnp.float32)).astype(jnp.bfloat16)
        both = jnp.concatenate([high, low], 1)
        rim = jnp.dot(rim_sel, both, preferred_element_type=jnp.float32)
        rim = rim[:, :state_count] + rim[:, state_count:]
        from_prev = ring(rim[face_count:], "dom", 1)
        from_next = ring(rim[:face_count], "dom", -1)
        main = jnp.dot(scatter_sel, both, preferred_element_type=jnp.float32)
        main = main[:, :state_count] + main[:, state_count:]
        own = main[:node_count] + split_dot(face_put, from_prev)
        ghost = main[node_count:] + from_next
        summed = jnp.concatenate([own, ghost], 0)
        return wide_mass[:, None] * summed + wide_potential[:, None] * field_in

    def scaled_step(field_in):
        return (operate(field_in) - centre * field_in) / half_span

    previous = field_start
    current = scaled_step(field_start)
    for repeat in range(POLY - 1):
        previous, current = (current, 2.0 * scaled_step(current) - previous)
    filtered = current[:node_count].astype(jnp.bfloat16)
    position = lax.axis_index("st") % 4
    first_bit, second_bit = (1, 0)

    def rows_for(member):
        return lax.dynamic_slice_in_dim(rotation, member * state_count, state_count, 0)

    partner = from_partner(filtered, "st", first_bit)
    rotated = jnp.dot(filtered, rows_for(position), preferred_element_type=jnp.float32)
    rotated = rotated + jnp.dot(
        partner, rows_for(position ^ 1 << first_bit), preferred_element_type=jnp.float32
    )
    far_pair = from_partner(jnp.stack([filtered, partner], 0), "st", second_bit)
    rotated = rotated + jnp.dot(
        far_pair[0], rows_for(position ^ 1 << second_bit), preferred_element_type=jnp.float32
    )
    rotated = rotated + jnp.dot(
        far_pair[1], rows_for(position ^ 3), preferred_element_type=jnp.float32
    )
    return rotated


def solution(mesh):
    return jax.shard_map(
        body,
        mesh=mesh,
        in_specs=(P("dom", "st"), P("dom"), P("dom"), P(), P("dom", None), P("dom"), P(None, "st")),
        out_specs=P("dom", "st"),
        check_vma=False,
    )
```

```python
import jax
import jax.numpy as jnp
from jax import lax
from jax.sharding import PartitionSpec as P

POLY = 3


centre = 10.0
half_span = 10.0


def ring(block, axis, step):
    count = lax.axis_size(axis)
    route = [(i, (i + step) % count) for i in range(count)]
    return lax.ppermute(block, axis, route)


def from_partner(block, axis, distance):
    count = lax.axis_size(axis)
    route = []
    for low in range(count):
        high = low | 1 << distance
        if high != low and high < count:
            route += [(low, high), (high, low)]
    return lax.ppermute(block, axis, route)


def high_low(value):
    high = lax.reduce_precision(value, exponent_bits=8, mantissa_bits=7)
    low = value - high
    return jnp.concatenate([high.astype(jnp.bfloat16), low.astype(jnp.bfloat16)], 1)


def summed_halves(both):
    width = both.shape[1] // 2
    return both[:, :width] + both[:, width:]


def body(states, inv_mass, potential, cell_matrix, connect, face_rows, rotation):
    node_count, state_count = states.shape
    cell_count, cell_size = connect.shape
    face_count = face_rows.shape[0]
    wide_count = node_count + face_count
    pad = (-cell_size) % 16
    padded_size = cell_size + pad
    cell_rows = jnp.pad(connect, ((0, 0), (0, pad)), constant_values=-1).reshape(-1)
    padded_matrix = jnp.pad(cell_matrix, ((0, pad), (0, pad)))
    wide_ids = lax.broadcasted_iota(jnp.int32, (wide_count, 1), 0)
    gather_sel = (cell_rows[:, None] == wide_ids[:, 0][None, :]).astype(jnp.bfloat16)
    scatter_sel = (wide_ids == cell_rows[None, :]).astype(jnp.bfloat16)
    face_sel = (face_rows[:, None] == cell_rows[None, :]).astype(jnp.bfloat16)
    rim_sel = jnp.concatenate([face_sel, scatter_sel[node_count:]], 0)
    face_put = (wide_ids[:node_count] == face_rows[None, :]).astype(jnp.bfloat16)
    face_take = (face_rows[:, None] == wide_ids[:node_count, 0][None, :]).astype(jnp.bfloat16)

    face_states = jnp.dot(face_take, states, preferred_element_type=jnp.float32)
    mass_potential = jnp.stack([inv_mass, potential], 1)[face_rows]
    ghost = ring(jnp.concatenate([face_states, mass_potential], 1), "dom", -1)
    field_start = jnp.concatenate([states.astype(jnp.float32), ghost[:, :state_count]], 0)
    wide_mass = jnp.concatenate([inv_mass, ghost[:, state_count]], 0)
    wide_potential = jnp.concatenate([potential, ghost[:, state_count + 1]], 0)

    def operate(field_in, last):
        weighted = (wide_mass[:, None] * field_in).astype(jnp.bfloat16)
        values = jnp.dot(gather_sel, weighted, preferred_element_type=jnp.float32)
        values = values.astype(jnp.bfloat16).reshape(cell_count, padded_size, state_count)
        products = jnp.einsum(
            "ij,cjb->cib", padded_matrix, values, preferred_element_type=jnp.float32
        ).reshape(-1, state_count)
        both = high_low(products)
        rim = summed_halves(jnp.dot(rim_sel, both, preferred_element_type=jnp.float32))
        from_prev = ring(rim[face_count:], "dom", 1)
        if last:
            main = summed_halves(
                jnp.dot(scatter_sel[:node_count], both, preferred_element_type=jnp.float32)
            )
            own = main + summed_halves(
                jnp.dot(face_put, high_low(from_prev), preferred_element_type=jnp.float32)
            )
            rows = node_count
            return wide_mass[:rows, None] * own + wide_potential[:rows, None] * field_in[:rows]
        from_next = ring(rim[:face_count], "dom", -1)
        main = summed_halves(jnp.dot(scatter_sel, both, preferred_element_type=jnp.float32))
        own = main[:node_count] + summed_halves(
            jnp.dot(face_put, high_low(from_prev), preferred_element_type=jnp.float32)
        )
        summed = jnp.concatenate([own, main[node_count:] + from_next], 0)
        return wide_mass[:, None] * summed + wide_potential[:, None] * field_in

    def scaled_step(field_in, last=False):
        rows = node_count if last else wide_count
        return (operate(field_in, last) - centre * field_in[:rows]) / half_span

    previous = field_start
    current = scaled_step(field_start)
    for repeat in range(POLY - 1):
        last = repeat == POLY - 2
        rows = node_count if last else wide_count
        previous, current = (current, 2.0 * scaled_step(current, last) - previous[:rows])
    filtered = current[:node_count].astype(jnp.bfloat16)
    position = lax.axis_index("st") % 4

    def rows_for(member):
        return lax.dynamic_slice_in_dim(rotation, member * state_count, state_count, 0)

    across = from_partner(filtered, "st", 1)
    beside = from_partner(filtered, "st", 0)
    diagonal = from_partner(across, "st", 0)
    rotated = jnp.dot(filtered, rows_for(position), preferred_element_type=jnp.float32)
    rotated = rotated + jnp.dot(beside, rows_for(position ^ 1), preferred_element_type=jnp.float32)
    rotated = rotated + jnp.dot(across, rows_for(position ^ 2), preferred_element_type=jnp.float32)
    rotated = rotated + jnp.dot(
        diagonal, rows_for(position ^ 3), preferred_element_type=jnp.float32
    )
    return rotated


def solution(mesh):
    return jax.shard_map(
        body,
        mesh=mesh,
        in_specs=(P("dom", "st"), P("dom"), P("dom"), P(), P("dom", None), P("dom"), P(None, "st")),
        out_specs=P("dom", "st"),
        check_vma=False,
    )
```

```python
import jax
import jax.numpy as jnp
from jax import lax
from jax.sharding import PartitionSpec as P

POLY = 3


centre = 10.0
half_span = 10.0


def ring(block, axis, step):
    count = lax.axis_size(axis)
    route = [(i, (i + step) % count) for i in range(count)]
    return lax.ppermute(block, axis, route)


def from_partner(block, axis, distance):
    count = lax.axis_size(axis)
    route = []
    for low in range(count):
        high = low | 1 << distance
        if high != low and high < count:
            route += [(low, high), (high, low)]
    return lax.ppermute(block, axis, route)


def high_low(value):
    high = lax.reduce_precision(value, exponent_bits=8, mantissa_bits=7)
    low = value - high
    return jnp.concatenate([high.astype(jnp.bfloat16), low.astype(jnp.bfloat16)], 1)


def summed_halves(both):
    width = both.shape[1] // 2
    return both[:, :width] + both[:, width:]


def body(states, inv_mass, potential, cell_matrix, connect, face_rows, rotation):
    node_count, state_count = states.shape
    cell_count, cell_size = connect.shape
    face_count = face_rows.shape[0]
    wide_count = node_count + face_count
    pad = (-cell_size) % 16
    padded_size = cell_size + pad
    cell_rows = jnp.pad(connect, ((0, 0), (0, pad)), constant_values=-1).reshape(-1)
    padded_matrix = jnp.pad(cell_matrix, ((0, pad), (0, pad)))
    wide_ids = lax.broadcasted_iota(jnp.int32, (wide_count, 1), 0)
    gather_sel = (cell_rows[:, None] == wide_ids[:, 0][None, :]).astype(jnp.bfloat16)
    scatter_sel = (wide_ids == cell_rows[None, :]).astype(jnp.bfloat16)
    rim_ids = jnp.concatenate([face_rows, wide_ids[node_count:, 0]], 0)
    rim_sel = (rim_ids[:, None] == cell_rows[None, :]).astype(jnp.bfloat16)
    face_put = (wide_ids[:node_count] == face_rows[None, :]).astype(jnp.bfloat16)
    face_take = (face_rows[:, None] == wide_ids[:node_count, 0][None, :]).astype(jnp.bfloat16)

    face_states = jnp.dot(face_take, states, preferred_element_type=jnp.float32)
    mass_potential = jnp.stack([inv_mass, potential], 1)[face_rows]
    ghost = ring(jnp.concatenate([face_states, mass_potential], 1), "dom", -1)
    field_start = jnp.concatenate([states.astype(jnp.float32), ghost[:, :state_count]], 0)
    wide_mass = jnp.concatenate([inv_mass, ghost[:, state_count]], 0)
    wide_potential = jnp.concatenate([potential, ghost[:, state_count + 1]], 0)

    def operate(field_in):
        weighted = (wide_mass[:, None] * field_in).astype(jnp.bfloat16)
        values = jnp.dot(gather_sel, weighted, preferred_element_type=jnp.float32)
        values = values.astype(jnp.bfloat16).reshape(cell_count, padded_size, state_count)
        products = jnp.einsum(
            "ij,cjb->cib", padded_matrix, values, preferred_element_type=jnp.float32
        ).reshape(-1, state_count)
        both = high_low(products)
        rim = summed_halves(jnp.dot(rim_sel, both, preferred_element_type=jnp.float32))
        from_prev = ring(rim[face_count:], "dom", 1)
        from_next = ring(rim[:face_count], "dom", -1)
        main = summed_halves(jnp.dot(scatter_sel, both, preferred_element_type=jnp.float32))
        own = main[:node_count] + summed_halves(
            jnp.dot(face_put, high_low(from_prev), preferred_element_type=jnp.float32)
        )
        summed = jnp.concatenate([own, main[node_count:] + from_next], 0)
        return wide_mass[:, None] * summed + wide_potential[:, None] * field_in

    def chebyshev_step(step, carry):
        previous, current = carry
        scaled = (operate(current) - centre * current) / half_span
        first = step == 0
        gain = jnp.where(first, 1.0, 2.0).astype(jnp.float32)
        keep = jnp.where(first, 0.0, 1.0).astype(jnp.float32)
        return current, gain * scaled - keep * previous

    previous, current = lax.fori_loop(0, POLY, chebyshev_step, (field_start, field_start))
    filtered = current[:node_count].astype(jnp.bfloat16)
    position = lax.axis_index("st") % 4

    def rows_for(member):
        return lax.dynamic_slice_in_dim(rotation, member * state_count, state_count, 0)

    across = from_partner(filtered, "st", 1)
    beside = from_partner(filtered, "st", 0)
    diagonal = from_partner(across, "st", 0)
    rotated = jnp.dot(filtered, rows_for(position), preferred_element_type=jnp.float32)
    rotated = rotated + jnp.dot(beside, rows_for(position ^ 1), preferred_element_type=jnp.float32)
    rotated = rotated + jnp.dot(across, rows_for(position ^ 2), preferred_element_type=jnp.float32)
    rotated = rotated + jnp.dot(
        diagonal, rows_for(position ^ 3), preferred_element_type=jnp.float32
    )
    return rotated


def solution(mesh):
    return jax.shard_map(
        body,
        mesh=mesh,
        in_specs=(P("dom", "st"), P("dom"), P("dom"), P(), P("dom", None), P("dom"), P(None, "st")),
        out_specs=P("dom", "st"),
        check_vma=False,
    )
```

```python
import jax
import jax.numpy as jnp
from jax import lax
from jax.sharding import PartitionSpec as P

POLY = 3


centre = 10.0
half_span = 10.0


def ring(block, axis, step):
    count = lax.axis_size(axis)
    route = [(i, (i + step) % count) for i in range(count)]
    return lax.ppermute(block, axis, route)


def from_partner(block, axis, distance):
    count = lax.axis_size(axis)
    route = []
    for low in range(count):
        high = low | 1 << distance
        if high != low and high < count:
            route += [(low, high), (high, low)]
    return lax.ppermute(block, axis, route)


def high_low(value):
    high = lax.reduce_precision(value, exponent_bits=8, mantissa_bits=7)
    low = value - high
    return jnp.concatenate([high.astype(jnp.bfloat16), low.astype(jnp.bfloat16)], 1)


def summed_halves(both):
    width = both.shape[1] // 2
    return both[:, :width] + both[:, width:]


def body(states, inv_mass, potential, cell_matrix, connect, face_rows, rotation):
    node_count, state_count = states.shape
    cell_count, cell_size = connect.shape
    face_count = face_rows.shape[0]
    wide_count = node_count + face_count
    pad = (-cell_size) % 16
    padded_size = cell_size + pad
    cell_rows = jnp.pad(connect, ((0, 0), (0, pad)), constant_values=-1).reshape(-1)
    padded_matrix = jnp.pad(cell_matrix, ((0, pad), (0, pad)))
    wide_ids = lax.broadcasted_iota(jnp.int32, (wide_count, 1), 0)
    gather_sel = (cell_rows[:, None] == wide_ids[:, 0][None, :]).astype(jnp.bfloat16)
    scatter_sel = (wide_ids == cell_rows[None, :]).astype(jnp.bfloat16)
    rim_ids = jnp.concatenate([face_rows, wide_ids[node_count:, 0]], 0)
    rim_sel = (rim_ids[:, None] == cell_rows[None, :]).astype(jnp.bfloat16)
    face_put = (wide_ids[:node_count] == face_rows[None, :]).astype(jnp.bfloat16)
    face_take = (face_rows[:, None] == wide_ids[:node_count, 0][None, :]).astype(jnp.bfloat16)

    face_states = jnp.dot(face_take, states, preferred_element_type=jnp.float32)
    mass_potential = jnp.stack([inv_mass, potential], 1)[face_rows]
    ghost = ring(jnp.concatenate([face_states, mass_potential], 1), "dom", -1)
    field_start = jnp.concatenate([states.astype(jnp.float32), ghost[:, :state_count]], 0)
    wide_mass = jnp.concatenate([inv_mass, ghost[:, state_count]], 0)
    wide_potential = jnp.concatenate([potential, ghost[:, state_count + 1]], 0)

    def operate(field_in):
        weighted = (wide_mass[:, None] * field_in).astype(jnp.bfloat16)
        values = jnp.dot(gather_sel, weighted, preferred_element_type=jnp.float32)
        values = values.astype(jnp.bfloat16).reshape(cell_count, padded_size, state_count)
        products = jnp.einsum(
            "ij,cjb->cib", padded_matrix, values, preferred_element_type=jnp.float32
        ).reshape(-1, state_count)
        both = high_low(products)
        rim = summed_halves(jnp.dot(rim_sel, both, preferred_element_type=jnp.float32))
        from_prev = ring(rim[face_count:], "dom", 1)
        from_next = ring(rim[:face_count], "dom", -1)
        main = summed_halves(jnp.dot(scatter_sel, both, preferred_element_type=jnp.float32))
        own = main[:node_count] + summed_halves(
            jnp.dot(face_put, high_low(from_prev), preferred_element_type=jnp.float32)
        )
        summed = jnp.concatenate([own, main[node_count:] + from_next], 0)
        return wide_mass[:, None] * summed + wide_potential[:, None] * field_in

    def chebyshev_step(step, carry):
        previous, current = carry
        scaled = (operate(current) - centre * current) / half_span
        first = step == 0
        gain = jnp.where(first, 1.0, 2.0).astype(jnp.float32)
        keep = jnp.where(first, 0.0, 1.0).astype(jnp.float32)
        return current, gain * scaled - keep * previous

    previous, current = lax.fori_loop(
        0, POLY - 1, chebyshev_step, (field_start, field_start)
    )

    weighted = (wide_mass[:, None] * current).astype(jnp.bfloat16)
    values = jnp.dot(gather_sel, weighted, preferred_element_type=jnp.float32)
    values = values.astype(jnp.bfloat16).reshape(cell_count, padded_size, state_count)
    products = jnp.einsum(
        "ij,cjb->cib", padded_matrix, values, preferred_element_type=jnp.float32
    ).reshape(-1, state_count)
    both = high_low(products)
    ghost_part = summed_halves(
        jnp.dot(rim_sel[face_count:], both, preferred_element_type=jnp.float32)
    )
    from_prev = high_low(ring(ghost_part, "dom", 1))
    chunks = 2 if node_count % 32 == 0 else 1
    chunk = node_count // chunks
    position = lax.axis_index("st") % 4

    def rows_for(member):
        return lax.dynamic_slice_in_dim(rotation, member * state_count, state_count, 0)

    pieces = []
    chunk_both = both
    for part in range(chunks):
        rows = slice(part * chunk, (part + 1) * chunk)
        main = summed_halves(
            jnp.dot(scatter_sel[rows], chunk_both, preferred_element_type=jnp.float32)
        )
        own = main + summed_halves(
            jnp.dot(face_put[rows], from_prev, preferred_element_type=jnp.float32)
        )
        field = current[rows]
        applied = wide_mass[rows, None] * own + wide_potential[rows, None] * field
        scaled = (applied - centre * field) / half_span
        filtered = (2.0 * scaled - previous[rows]).astype(jnp.bfloat16)
        filtered, chunk_both = lax.optimization_barrier((filtered, both))
        across = from_partner(filtered, "st", 1)
        beside = from_partner(filtered, "st", 0)
        diagonal = from_partner(across, "st", 0)
        rotated = jnp.dot(filtered, rows_for(position), preferred_element_type=jnp.float32)
        rotated = rotated + jnp.dot(
            beside, rows_for(position ^ 1), preferred_element_type=jnp.float32
        )
        rotated = rotated + jnp.dot(
            across, rows_for(position ^ 2), preferred_element_type=jnp.float32
        )
        rotated = rotated + jnp.dot(
            diagonal, rows_for(position ^ 3), preferred_element_type=jnp.float32
        )
        pieces.append(rotated)
    return jnp.concatenate(pieces, 0)


def solution(mesh):
    return jax.shard_map(
        body,
        mesh=mesh,
        in_specs=(P("dom", "st"), P("dom"), P("dom"), P(), P("dom", None), P("dom"), P(None, "st")),
        out_specs=P("dom", "st"),
        check_vma=False,
    )
```

```python
import jax
import jax.numpy as jnp
from jax import lax
from jax.sharding import PartitionSpec as P

POLY = 3


centre = 10.0
half_span = 10.0


def ring(block, axis, step):
    count = lax.axis_size(axis)
    route = [(i, (i + step) % count) for i in range(count)]
    return lax.ppermute(block, axis, route)


def from_partner(block, axis, distance):
    count = lax.axis_size(axis)
    route = []
    for low in range(count):
        high = low | 1 << distance
        if high != low and high < count:
            route += [(low, high), (high, low)]
    return lax.ppermute(block, axis, route)


def high_low(value):
    high = lax.reduce_precision(value, exponent_bits=8, mantissa_bits=7)
    low = value - high
    return jnp.concatenate([high.astype(jnp.bfloat16), low.astype(jnp.bfloat16)], 1)


def summed_halves(both):
    width = both.shape[1] // 2
    return both[:, :width] + both[:, width:]


def body(states, inv_mass, potential, cell_matrix, connect, face_rows, rotation):
    node_count, state_count = states.shape
    cell_count, cell_size = connect.shape
    face_count = face_rows.shape[0]
    wide_count = node_count + face_count
    pad = (-cell_size) % 16
    padded_size = cell_size + pad
    cell_rows = jnp.pad(connect, ((0, 0), (0, pad)), constant_values=-1).reshape(-1)
    padded_matrix = jnp.pad(cell_matrix, ((0, pad), (0, pad)))
    wide_ids = lax.broadcasted_iota(jnp.int32, (wide_count, 1), 0)
    gather_sel = (cell_rows[:, None] == wide_ids[:, 0][None, :]).astype(jnp.bfloat16)
    scatter_sel = (wide_ids == cell_rows[None, :]).astype(jnp.bfloat16)
    rim_ids = jnp.concatenate([face_rows, wide_ids[node_count:, 0]], 0)
    rim_sel = (rim_ids[:, None] == cell_rows[None, :]).astype(jnp.bfloat16)
    face_put = (wide_ids[:node_count] == face_rows[None, :]).astype(jnp.bfloat16)
    face_take = (face_rows[:, None] == wide_ids[:node_count, 0][None, :]).astype(jnp.bfloat16)

    face_states = jnp.dot(face_take, states, preferred_element_type=jnp.float32)
    face_mass_potential = jnp.stack([inv_mass, potential], 0)[:, face_rows]
    ghost_states, ghost_mass_potential = ring((face_states, face_mass_potential), "dom", -1)
    field_start = jnp.concatenate([states.astype(jnp.float32), ghost_states], 0)
    wide_mass = jnp.concatenate([inv_mass, ghost_mass_potential[0]], 0)
    wide_potential = jnp.concatenate([potential, ghost_mass_potential[1]], 0)

    def operate(field_in, values=None):
        if values is None:
            weighted = (wide_mass[:, None] * field_in).astype(jnp.bfloat16)
            values = jnp.dot(gather_sel, weighted, preferred_element_type=jnp.float32)
        values = values.astype(jnp.bfloat16).reshape(cell_count, padded_size, state_count)
        products = jnp.einsum(
            "ij,cjb->cib", padded_matrix, values, preferred_element_type=jnp.float32
        ).reshape(-1, state_count)
        both = high_low(products)
        rim = summed_halves(jnp.dot(rim_sel, both, preferred_element_type=jnp.float32))
        from_prev = ring(rim[face_count:], "dom", 1)
        from_next = ring(rim[:face_count], "dom", -1)
        main = summed_halves(jnp.dot(scatter_sel, both, preferred_element_type=jnp.float32))
        own = main[:node_count] + summed_halves(
            jnp.dot(face_put, high_low(from_prev), preferred_element_type=jnp.float32)
        )
        summed = jnp.concatenate([own, main[node_count:] + from_next], 0)
        return wide_mass[:, None] * summed + wide_potential[:, None] * field_in

    def chebyshev_step(step, carry):
        previous, current = carry
        scaled = (operate(current) - centre * current) / half_span
        first = step == 0
        gain = jnp.where(first, 1.0, 2.0).astype(jnp.float32)
        keep = jnp.where(first, 0.0, 1.0).astype(jnp.float32)
        return current, gain * scaled - keep * previous

    local_weighted = (inv_mass[:, None] * states.astype(jnp.float32)).astype(jnp.bfloat16)
    ghost_weighted = (ghost_mass_potential[0][:, None] * ghost_states).astype(jnp.bfloat16)
    first_values = jnp.dot(
        gather_sel[:, :node_count], local_weighted, preferred_element_type=jnp.float32
    ) + jnp.dot(gather_sel[:, node_count:], ghost_weighted, preferred_element_type=jnp.float32)
    first = (operate(field_start, first_values) - centre * field_start) / half_span
    previous, current = lax.fori_loop(1, POLY, chebyshev_step, (field_start, first))
    filtered = current[:node_count].astype(jnp.bfloat16)
    position = lax.axis_index("st") % 4

    def rows_for(member):
        return lax.dynamic_slice_in_dim(rotation, member * state_count, state_count, 0)

    across = from_partner(filtered, "st", 1)
    beside = from_partner(filtered, "st", 0)
    diagonal = from_partner(across, "st", 0)
    rotated = jnp.dot(filtered, rows_for(position), preferred_element_type=jnp.float32)
    rotated = rotated + jnp.dot(beside, rows_for(position ^ 1), preferred_element_type=jnp.float32)
    rotated = lax.optimization_barrier(rotated)
    rotated = rotated + jnp.dot(across, rows_for(position ^ 2), preferred_element_type=jnp.float32)
    rotated = rotated + jnp.dot(
        diagonal, rows_for(position ^ 3), preferred_element_type=jnp.float32
    )
    return rotated


def solution(mesh):
    return jax.shard_map(
        body,
        mesh=mesh,
        in_specs=(P("dom", "st"), P("dom"), P("dom"), P(), P("dom", None), P("dom"), P(None, "st")),
        out_specs=P("dom", "st"),
        check_vma=False,
    )
```

```python
import jax
import jax.numpy as jnp
from jax import lax
from jax.sharding import PartitionSpec as P

POLY = 3


centre = 10.0
half_span = 10.0


def ring(block, axis, step):
    count = lax.axis_size(axis)
    route = [(i, (i + step) % count) for i in range(count)]
    return lax.ppermute(block, axis, route)


def from_partner(block, axis, distance):
    count = lax.axis_size(axis)
    route = []
    for low in range(count):
        high = low | 1 << distance
        if high != low and high < count:
            route += [(low, high), (high, low)]
    return lax.ppermute(block, axis, route)


def high_low(value):
    high = lax.reduce_precision(value, exponent_bits=8, mantissa_bits=7)
    low = value - high
    return jnp.concatenate([high.astype(jnp.bfloat16), low.astype(jnp.bfloat16)], 1)


def summed_halves(both):
    width = both.shape[1] // 2
    return both[:, :width] + both[:, width:]


def body(states, inv_mass, potential, cell_matrix, connect, face_rows, rotation):
    node_count, state_count = states.shape
    cell_count, cell_size = connect.shape
    face_count = face_rows.shape[0]
    wide_count = node_count + face_count
    pad = (-cell_size) % 16
    padded_size = cell_size + pad
    cell_rows = jnp.pad(connect, ((0, 0), (0, pad)), constant_values=-1).reshape(-1)
    padded_matrix = jnp.pad(cell_matrix, ((0, pad), (0, pad)))
    wide_ids = lax.broadcasted_iota(jnp.int32, (wide_count, 1), 0)
    gather_sel = (cell_rows[:, None] == wide_ids[:, 0][None, :]).astype(jnp.bfloat16)
    scatter_sel = (wide_ids == cell_rows[None, :]).astype(jnp.bfloat16)
    rim_ids = jnp.concatenate([face_rows, wide_ids[node_count:, 0]], 0)
    rim_sel = (rim_ids[:, None] == cell_rows[None, :]).astype(jnp.bfloat16)
    face_put = (wide_ids[:node_count] == face_rows[None, :]).astype(jnp.bfloat16)
    face_take = (face_rows[:, None] == wide_ids[:node_count, 0][None, :]).astype(jnp.bfloat16)

    face_states = jnp.dot(face_take, states, preferred_element_type=jnp.float32)
    mass_potential = jnp.stack([inv_mass, potential], 1)[face_rows]
    ghost = ring(jnp.concatenate([face_states, mass_potential], 1), "dom", -1)
    field_start = jnp.concatenate([states.astype(jnp.float32), ghost[:, :state_count]], 0)
    wide_mass = jnp.concatenate([inv_mass, ghost[:, state_count]], 0)
    wide_potential = jnp.concatenate([potential, ghost[:, state_count + 1]], 0)

    def operate(field_in):
        weighted = (wide_mass[:, None] * field_in).astype(jnp.bfloat16)
        values = lax.dot_general(
            scatter_sel, weighted, (((0,), (0,)), ((), ())), preferred_element_type=jnp.float32
        )
        values = values.astype(jnp.bfloat16).reshape(cell_count, padded_size, state_count)
        products = jnp.einsum(
            "ij,cjb->cib", padded_matrix, values, preferred_element_type=jnp.float32
        ).reshape(-1, state_count)
        both = high_low(products)
        rim = summed_halves(jnp.dot(rim_sel, both, preferred_element_type=jnp.float32))
        from_prev = ring(rim[face_count:], "dom", 1)
        from_next = ring(rim[:face_count], "dom", -1)
        main = summed_halves(jnp.dot(scatter_sel, both, preferred_element_type=jnp.float32))
        own = main[:node_count] + summed_halves(
            jnp.dot(face_put, high_low(from_prev), preferred_element_type=jnp.float32)
        )
        summed = jnp.concatenate([own, main[node_count:] + from_next], 0)
        return wide_mass[:, None] * summed + wide_potential[:, None] * field_in

    def chebyshev_step(step, carry):
        previous, current = carry
        scaled = (operate(current) - centre * current) / half_span
        first = step == 0
        gain = jnp.where(first, 1.0, 2.0).astype(jnp.float32)
        keep = jnp.where(first, 0.0, 1.0).astype(jnp.float32)
        return current, gain * scaled - keep * previous

    previous, current = lax.fori_loop(0, POLY, chebyshev_step, (field_start, field_start))
    filtered = current[:node_count].astype(jnp.bfloat16)
    position = lax.axis_index("st") % 4

    def rows_for(member):
        return lax.dynamic_slice_in_dim(rotation, member * state_count, state_count, 0)

    across = from_partner(filtered, "st", 1)
    beside = from_partner(filtered, "st", 0)
    diagonal = from_partner(across, "st", 0)
    rotated = jnp.dot(filtered, rows_for(position), preferred_element_type=jnp.float32)
    rotated = rotated + jnp.dot(beside, rows_for(position ^ 1), preferred_element_type=jnp.float32)
    rotated = rotated + jnp.dot(across, rows_for(position ^ 2), preferred_element_type=jnp.float32)
    rotated = rotated + jnp.dot(
        diagonal, rows_for(position ^ 3), preferred_element_type=jnp.float32
    )
    return rotated


def solution(mesh):
    return jax.shard_map(
        body,
        mesh=mesh,
        in_specs=(P("dom", "st"), P("dom"), P("dom"), P(), P("dom", None), P("dom"), P(None, "st")),
        out_specs=P("dom", "st"),
        check_vma=False,
    )
```

```python
import jax
import jax.numpy as jnp
from jax import lax
from jax.sharding import PartitionSpec as P

POLY = 3


centre = 10.0
half_span = 10.0


def ring(block, axis, step):
    count = lax.axis_size(axis)
    route = [(i, (i + step) % count) for i in range(count)]
    return lax.ppermute(block, axis, route)


def from_partner(block, axis, distance):
    count = lax.axis_size(axis)
    route = []
    for low in range(count):
        high = low | 1 << distance
        if high != low and high < count:
            route += [(low, high), (high, low)]
    return lax.ppermute(block, axis, route)


def high_low(value):
    high = lax.reduce_precision(value, exponent_bits=8, mantissa_bits=7)
    low = value - high
    return jnp.concatenate([high.astype(jnp.bfloat16), low.astype(jnp.bfloat16)], 1)


def summed_halves(both):
    width = both.shape[1] // 2
    return both[:, :width] + both[:, width:]


def body(states, inv_mass, potential, cell_matrix, connect, face_rows, rotation):
    node_count, state_count = states.shape
    cell_count, cell_size = connect.shape
    face_count = face_rows.shape[0]
    wide_count = node_count + face_count
    pad = (-cell_size) % 16
    padded_size = cell_size + pad
    cell_rows = jnp.pad(connect, ((0, 0), (0, pad)), constant_values=-1).reshape(-1)
    padded_matrix = jnp.pad(cell_matrix, ((0, pad), (0, pad)))
    wide_ids = lax.broadcasted_iota(jnp.int32, (wide_count, 1), 0)
    gather_sel = (cell_rows[:, None] == wide_ids[:, 0][None, :]).astype(jnp.bfloat16)
    scatter_sel = (wide_ids == cell_rows[None, :]).astype(jnp.bfloat16)
    rim_ids = jnp.concatenate([face_rows, wide_ids[node_count:, 0]], 0)
    rim_sel = (rim_ids[:, None] == cell_rows[None, :]).astype(jnp.bfloat16)
    face_put = (wide_ids[:node_count] == face_rows[None, :]).astype(jnp.bfloat16)

    face_states = lax.dot_general(
        face_put, states, (((0,), (0,)), ((), ())), preferred_element_type=jnp.float32
    )
    mass_potential = jnp.stack([inv_mass, potential], 1).at[face_rows].get(
        mode="promise_in_bounds"
    )
    rim_cells = rim_sel.reshape(2 * face_count, cell_count, padded_size)
    rim_matrix = jnp.einsum(
        "rci,ij->rcj", rim_cells, padded_matrix, preferred_element_type=jnp.float32
    ).reshape(2 * face_count, -1)
    rim_high = lax.reduce_precision(rim_matrix, exponent_bits=8, mantissa_bits=7)
    rim_both = jnp.concatenate(
        [rim_high.astype(jnp.bfloat16), (rim_matrix - rim_high).astype(jnp.bfloat16)], 0
    )
    ghost = ring(jnp.concatenate([face_states, mass_potential], 1), "dom", -1)
    field_start = jnp.concatenate([states.astype(jnp.float32), ghost[:, :state_count]], 0)
    wide_mass = jnp.concatenate([inv_mass, ghost[:, state_count]], 0)
    wide_potential = jnp.concatenate([potential, ghost[:, state_count + 1]], 0)

    def operate(field_in):
        weighted = (wide_mass[:, None] * field_in).astype(jnp.bfloat16)
        values = lax.dot_general(
            scatter_sel, weighted, (((0,), (0,)), ((), ())), preferred_element_type=jnp.float32
        )
        values = values.astype(jnp.bfloat16).reshape(cell_count, padded_size, state_count)
        products = jnp.einsum(
            "ij,cjb->cib", padded_matrix, values, preferred_element_type=jnp.float32
        ).reshape(-1, state_count)
        both = high_low(products)
        rim_two = jnp.dot(rim_both, values.reshape(-1, state_count), preferred_element_type=jnp.float32)
        rim = rim_two[: 2 * face_count] + rim_two[2 * face_count :]
        from_prev = ring(rim[face_count:], "dom", 1)
        from_next = ring(rim[:face_count], "dom", -1)
        main = summed_halves(jnp.dot(scatter_sel, both, preferred_element_type=jnp.float32))
        own = main[:node_count] + summed_halves(
            jnp.dot(face_put, high_low(from_prev), preferred_element_type=jnp.float32)
        )
        summed = jnp.concatenate([own, main[node_count:] + from_next], 0)
        return wide_mass[:, None] * summed + wide_potential[:, None] * field_in

    def chebyshev_step(step, carry):
        previous, current = carry
        scaled = (operate(current) - centre * current) / half_span
        first = step == 0
        gain = jnp.where(first, 1.0, 2.0).astype(jnp.float32)
        keep = jnp.where(first, 0.0, 1.0).astype(jnp.float32)
        return current, gain * scaled - keep * previous

    previous, current = lax.fori_loop(0, POLY, chebyshev_step, (field_start, field_start))
    filtered = current[:node_count].astype(jnp.bfloat16)
    position = lax.axis_index("st") % 4

    def rows_for(member):
        return lax.dynamic_slice_in_dim(rotation, member * state_count, state_count, 0)

    across = from_partner(filtered, "st", 1)
    beside = from_partner(filtered, "st", 0)
    diagonal = from_partner(across, "st", 0)
    rotated = jnp.dot(filtered, rows_for(position), preferred_element_type=jnp.float32)
    rotated = rotated + jnp.dot(beside, rows_for(position ^ 1), preferred_element_type=jnp.float32)
    rotated = rotated + jnp.dot(across, rows_for(position ^ 2), preferred_element_type=jnp.float32)
    rotated = rotated + jnp.dot(
        diagonal, rows_for(position ^ 3), preferred_element_type=jnp.float32
    )
    return rotated


def solution(mesh):
    return jax.shard_map(
        body,
        mesh=mesh,
        in_specs=(P("dom", "st"), P("dom"), P("dom"), P(), P("dom", None), P("dom"), P(None, "st")),
        out_specs=P("dom", "st"),
        check_vma=False,
    )
```

```python
import jax
import jax.numpy as jnp
from jax import lax
from jax.sharding import PartitionSpec as P

POLY = 3


centre = 10.0
half_span = 10.0


def ring(block, axis, step):
    count = lax.axis_size(axis)
    route = [(i, (i + step) % count) for i in range(count)]
    return lax.ppermute(block, axis, route)


def from_partner(block, axis, distance):
    count = lax.axis_size(axis)
    route = []
    for low in range(count):
        high = low | 1 << distance
        if high != low and high < count:
            route += [(low, high), (high, low)]
    return lax.ppermute(block, axis, route)


def high_low(value):
    high = lax.reduce_precision(value, exponent_bits=8, mantissa_bits=7)
    low = value - high
    return jnp.concatenate([high.astype(jnp.bfloat16), low.astype(jnp.bfloat16)], 1)


def summed_halves(both):
    width = both.shape[1] // 2
    return both[:, :width] + both[:, width:]


def body(states, inv_mass, potential, cell_matrix, connect, face_rows, rotation):
    node_count, state_count = states.shape
    cell_count, cell_size = connect.shape
    face_count = face_rows.shape[0]
    wide_count = node_count + face_count
    pad = (-cell_size) % 16
    padded_size = cell_size + pad
    cell_rows = jnp.pad(connect, ((0, 0), (0, pad)), constant_values=-1).reshape(-1)
    padded_matrix = jnp.pad(cell_matrix, ((0, pad), (0, pad)))
    wide_ids = lax.broadcasted_iota(jnp.int32, (wide_count, 1), 0)
    gather_sel = (cell_rows[:, None] == wide_ids[:, 0][None, :]).astype(jnp.bfloat16)
    scatter_sel = (wide_ids == cell_rows[None, :]).astype(jnp.bfloat16)
    rim_ids = jnp.concatenate([face_rows, wide_ids[node_count:, 0]], 0)
    rim_sel = (rim_ids[:, None] == cell_rows[None, :]).astype(jnp.bfloat16)
    face_put = (wide_ids[:node_count] == face_rows[None, :]).astype(jnp.bfloat16)
    face_take = (face_rows[:, None] == wide_ids[:node_count, 0][None, :]).astype(jnp.bfloat16)

    face_states = jnp.dot(face_take, states, preferred_element_type=jnp.float32)
    face_mass_potential = lax.dot_general(
        jnp.stack([inv_mass, potential], 0),
        face_put.astype(jnp.float32),
        (((1,), (0,)), ((), ())),
        precision=lax.Precision.HIGHEST,
        preferred_element_type=jnp.float32,
    )
    ghost_states, ghost_mass_potential = ring((face_states, face_mass_potential), "dom", -1)
    field_start = jnp.concatenate([states.astype(jnp.float32), ghost_states], 0)
    wide_mass = jnp.concatenate([inv_mass, ghost_mass_potential[0]], 0)
    wide_potential = jnp.concatenate([potential, ghost_mass_potential[1]], 0)

    def operate(field_in):
        weighted = (wide_mass[:, None] * field_in).astype(jnp.bfloat16)
        values = lax.dot_general(
            scatter_sel, weighted, (((0,), (0,)), ((), ())), preferred_element_type=jnp.float32
        )
        values = values.astype(jnp.bfloat16).reshape(cell_count, padded_size, state_count)
        products = jnp.einsum(
            "ij,cjb->cib", padded_matrix, values, preferred_element_type=jnp.float32
        ).reshape(-1, state_count)
        both = high_low(products)
        rim = summed_halves(jnp.dot(rim_sel, both, preferred_element_type=jnp.float32))
        from_prev = ring(rim[face_count:], "dom", 1)
        from_next = ring(rim[:face_count], "dom", -1)
        main = summed_halves(jnp.dot(scatter_sel, both, preferred_element_type=jnp.float32))
        own = main[:node_count] + summed_halves(
            jnp.dot(face_put, high_low(from_prev), preferred_element_type=jnp.float32)
        )
        summed = jnp.concatenate([own, main[node_count:] + from_next], 0)
        return wide_mass[:, None] * summed + wide_potential[:, None] * field_in

    def chebyshev_step(step, carry):
        previous, current = carry
        scaled = (operate(current) - centre * current) / half_span
        first = step == 0
        gain = jnp.where(first, 1.0, 2.0).astype(jnp.float32)
        keep = jnp.where(first, 0.0, 1.0).astype(jnp.float32)
        return current, gain * scaled - keep * previous

    previous, current = lax.fori_loop(0, POLY, chebyshev_step, (field_start, field_start))
    filtered = current[:node_count].astype(jnp.bfloat16)
    position = lax.axis_index("st") % 4

    def rows_for(member):
        return lax.dynamic_slice_in_dim(rotation, member * state_count, state_count, 0)

    across = from_partner(filtered, "st", 1)
    beside = from_partner(filtered, "st", 0)
    diagonal = from_partner(across, "st", 0)
    rotated = jnp.dot(filtered, rows_for(position), preferred_element_type=jnp.float32)
    rotated = rotated + jnp.dot(beside, rows_for(position ^ 1), preferred_element_type=jnp.float32)
    rotated = rotated + jnp.dot(across, rows_for(position ^ 2), preferred_element_type=jnp.float32)
    rotated = rotated + jnp.dot(
        diagonal, rows_for(position ^ 3), preferred_element_type=jnp.float32
    )
    return rotated


def solution(mesh):
    return jax.shard_map(
        body,
        mesh=mesh,
        in_specs=(P("dom", "st"), P("dom"), P("dom"), P(), P("dom", None), P("dom"), P(None, "st")),
        out_specs=P("dom", "st"),
        check_vma=False,
    )
```

```python
import jax
import jax.numpy as jnp
from jax import lax
from jax.sharding import PartitionSpec as P

POLY = 3


centre = 10.0
half_span = 10.0


def ring(block, axis, step):
    count = lax.axis_size(axis)
    route = [(i, (i + step) % count) for i in range(count)]
    return lax.ppermute(block, axis, route)


def from_partner(block, axis, distance):
    count = lax.axis_size(axis)
    route = []
    for low in range(count):
        high = low | 1 << distance
        if high != low and high < count:
            route += [(low, high), (high, low)]
    return lax.ppermute(block, axis, route)


def high_low(value):
    high = lax.reduce_precision(value, exponent_bits=8, mantissa_bits=7)
    low = value - high
    return jnp.concatenate([high.astype(jnp.bfloat16), low.astype(jnp.bfloat16)], 1)


def summed_halves(both):
    width = both.shape[1] // 2
    return both[:, :width] + both[:, width:]


def body(states, inv_mass, potential, cell_matrix, connect, face_rows, rotation):
    node_count, state_count = states.shape
    cell_count, cell_size = connect.shape
    face_count = face_rows.shape[0]
    wide_count = node_count + face_count
    pad = (-cell_size) % 16
    padded_size = cell_size + pad
    cell_rows = jnp.pad(connect, ((0, 0), (0, pad)), constant_values=-1).reshape(-1)
    padded_matrix = jnp.pad(cell_matrix, ((0, pad), (0, pad)))
    wide_ids = lax.broadcasted_iota(jnp.int32, (wide_count, 1), 0)
    gather_sel = (cell_rows[:, None] == wide_ids[:, 0][None, :]).astype(jnp.bfloat16)
    scatter_sel = (wide_ids == cell_rows[None, :]).astype(jnp.bfloat16)
    rim_ids = jnp.concatenate([face_rows, wide_ids[node_count:, 0]], 0)
    rim_sel = (rim_ids[:, None] == cell_rows[None, :]).astype(jnp.bfloat16)
    face_put = (wide_ids[:node_count] == face_rows[None, :]).astype(jnp.bfloat16)
    face_take = (face_rows[:, None] == wide_ids[:node_count, 0][None, :]).astype(jnp.bfloat16)

    face_states = jnp.dot(face_take, states, preferred_element_type=jnp.float32)
    face_mass_potential = lax.dot_general(
        jnp.stack([inv_mass, potential], 0),
        face_put.astype(jnp.float32),
        (((1,), (0,)), ((), ())),
        precision=lax.Precision.HIGHEST,
        preferred_element_type=jnp.float32,
    )
    face_states, face_mass_potential, local_start, padded_matrix = lax.optimization_barrier(
        (face_states, face_mass_potential, states.astype(jnp.float32), padded_matrix)
    )
    ghost_states, ghost_mass_potential = ring((face_states, face_mass_potential), "dom", -1)
    field_start = jnp.concatenate([local_start, ghost_states], 0)
    wide_mass = jnp.concatenate([inv_mass, ghost_mass_potential[0]], 0)
    wide_potential = jnp.concatenate([potential, ghost_mass_potential[1]], 0)

    def operate(field_in):
        weighted = (wide_mass[:, None] * field_in).astype(jnp.bfloat16)
        values = lax.dot_general(
            scatter_sel, weighted, (((0,), (0,)), ((), ())), preferred_element_type=jnp.float32
        )
        values = values.astype(jnp.bfloat16).reshape(cell_count, padded_size, state_count)
        products = jnp.einsum(
            "ij,cjb->cib", padded_matrix, values, preferred_element_type=jnp.float32
        ).reshape(-1, state_count)
        both = high_low(products)
        rim = summed_halves(jnp.dot(rim_sel, both, preferred_element_type=jnp.float32))
        from_prev = ring(rim[face_count:], "dom", 1)
        from_next = ring(rim[:face_count], "dom", -1)
        main = summed_halves(jnp.dot(scatter_sel, both, preferred_element_type=jnp.float32))
        own = main[:node_count] + summed_halves(
            jnp.dot(face_put, high_low(from_prev), preferred_element_type=jnp.float32)
        )
        summed = jnp.concatenate([own, main[node_count:] + from_next], 0)
        return wide_mass[:, None] * summed + wide_potential[:, None] * field_in

    def chebyshev_step(step, carry):
        previous, current = carry
        scaled = (operate(current) - centre * current) / half_span
        first = step == 0
        gain = jnp.where(first, 1.0, 2.0).astype(jnp.float32)
        keep = jnp.where(first, 0.0, 1.0).astype(jnp.float32)
        return current, gain * scaled - keep * previous

    previous, current = lax.fori_loop(0, POLY, chebyshev_step, (field_start, field_start))
    filtered = current[:node_count].astype(jnp.bfloat16)
    position = lax.axis_index("st") % 4

    def rows_for(member):
        return lax.dynamic_slice_in_dim(rotation, member * state_count, state_count, 0)

    across = from_partner(filtered, "st", 1)
    beside = from_partner(filtered, "st", 0)
    diagonal = from_partner(across, "st", 0)
    rotated = jnp.dot(filtered, rows_for(position), preferred_element_type=jnp.float32)
    rotated = rotated + jnp.dot(beside, rows_for(position ^ 1), preferred_element_type=jnp.float32)
    rotated = rotated + jnp.dot(across, rows_for(position ^ 2), preferred_element_type=jnp.float32)
    rotated = rotated + jnp.dot(
        diagonal, rows_for(position ^ 3), preferred_element_type=jnp.float32
    )
    return rotated


def solution(mesh):
    return jax.shard_map(
        body,
        mesh=mesh,
        in_specs=(P("dom", "st"), P("dom"), P("dom"), P(), P("dom", None), P("dom"), P(None, "st")),
        out_specs=P("dom", "st"),
        check_vma=False,
    )
```

```python
import jax
import jax.numpy as jnp
from jax import lax
from jax.sharding import PartitionSpec as P

POLY = 3


centre = 10.0
half_span = 10.0


def ring(block, axis, step):
    count = lax.axis_size(axis)
    route = [(i, (i + step) % count) for i in range(count)]
    return lax.ppermute(block, axis, route)


def from_partner(block, axis, distance):
    count = lax.axis_size(axis)
    route = []
    for low in range(count):
        high = low | 1 << distance
        if high != low and high < count:
            route += [(low, high), (high, low)]
    return lax.ppermute(block, axis, route)


def high_low(value):
    high = lax.reduce_precision(value, exponent_bits=8, mantissa_bits=7)
    low = value - high
    return jnp.concatenate([high.astype(jnp.bfloat16), low.astype(jnp.bfloat16)], 1)


def summed_halves(both):
    width = both.shape[1] // 2
    return both[:, :width] + both[:, width:]


def body(states, inv_mass, potential, cell_matrix, connect, face_rows, rotation):
    node_count, state_count = states.shape
    cell_count, cell_size = connect.shape
    face_count = face_rows.shape[0]
    wide_count = node_count + face_count
    pad = (-cell_size) % 16
    padded_size = cell_size + pad
    cell_rows = jnp.pad(connect, ((0, 0), (0, pad)), constant_values=-1).reshape(-1)
    padded_matrix = jnp.pad(cell_matrix, ((0, pad), (0, pad)))
    wide_ids = lax.broadcasted_iota(jnp.int32, (wide_count, 1), 0)
    gather_sel = (cell_rows[:, None] == wide_ids[:, 0][None, :]).astype(jnp.bfloat16)
    scatter_sel = (wide_ids == cell_rows[None, :]).astype(jnp.bfloat16)
    rim_ids = jnp.concatenate([face_rows, wide_ids[node_count:, 0]], 0)
    rim_sel = (rim_ids[:, None] == cell_rows[None, :]).astype(jnp.bfloat16)
    face_put = (wide_ids[:node_count] == face_rows[None, :]).astype(jnp.bfloat16)
    face_take = (face_rows[:, None] == wide_ids[:node_count, 0][None, :]).astype(jnp.bfloat16)

    face_states = jnp.dot(face_take, states, preferred_element_type=jnp.float32)
    face_mass_potential = lax.dot_general(
        jnp.stack([inv_mass, potential], 0),
        face_put.astype(jnp.float32),
        (((1,), (0,)), ((), ())),
        precision=lax.Precision.HIGHEST,
        preferred_element_type=jnp.float32,
    )
    ghost_states, ghost_mass_potential = ring((face_states, face_mass_potential), "dom", -1)
    field_start = jnp.concatenate([states.astype(jnp.float32), ghost_states], 0)
    wide_mass = jnp.concatenate([inv_mass, ghost_mass_potential[0]], 0)
    wide_potential = jnp.concatenate([potential, ghost_mass_potential[1]], 0)

    def operate(field_in):
        weighted = (wide_mass[:, None] * field_in).astype(jnp.bfloat16)
        values = lax.dot_general(
            scatter_sel, weighted, (((0,), (0,)), ((), ())), preferred_element_type=jnp.float32
        )
        values = values.astype(jnp.bfloat16).reshape(cell_count, padded_size, state_count)
        products = jnp.einsum(
            "ij,cjb->cib", padded_matrix, values, preferred_element_type=jnp.float32
        ).reshape(-1, state_count)
        both = high_low(products)
        rim = summed_halves(jnp.dot(rim_sel, both, preferred_element_type=jnp.float32))
        from_prev = ring(rim[face_count:], "dom", 1)
        from_next = ring(rim[:face_count], "dom", -1)
        main = summed_halves(jnp.dot(scatter_sel, both, preferred_element_type=jnp.float32))
        own = main[:node_count] + summed_halves(
            lax.dot_general(
                face_take, high_low(from_prev), (((0,), (0,)), ((), ())),
                preferred_element_type=jnp.float32,
            )
        )
        summed = jnp.concatenate([own, main[node_count:] + from_next], 0)
        return wide_mass[:, None] * summed + wide_potential[:, None] * field_in

    def chebyshev_step(step, carry):
        previous, current = carry
        scaled = (operate(current) - centre * current) / half_span
        first = step == 0
        gain = jnp.where(first, 1.0, 2.0).astype(jnp.float32)
        keep = jnp.where(first, 0.0, 1.0).astype(jnp.float32)
        return current, gain * scaled - keep * previous

    previous, current = lax.fori_loop(0, POLY, chebyshev_step, (field_start, field_start))
    filtered = current[:node_count].astype(jnp.bfloat16)
    position = lax.axis_index("st") % 4

    def rows_for(member):
        return lax.dynamic_slice_in_dim(rotation, member * state_count, state_count, 0)

    across = from_partner(filtered, "st", 1)
    beside = from_partner(filtered, "st", 0)
    diagonal = from_partner(across, "st", 0)
    rotated = jnp.dot(filtered, rows_for(position), preferred_element_type=jnp.float32)
    rotated = rotated + jnp.dot(beside, rows_for(position ^ 1), preferred_element_type=jnp.float32)
    rotated = rotated + jnp.dot(across, rows_for(position ^ 2), preferred_element_type=jnp.float32)
    rotated = rotated + jnp.dot(
        diagonal, rows_for(position ^ 3), preferred_element_type=jnp.float32
    )
    return rotated


def solution(mesh):
    return jax.shard_map(
        body,
        mesh=mesh,
        in_specs=(P("dom", "st"), P("dom"), P("dom"), P(), P("dom", None), P("dom"), P(None, "st")),
        out_specs=P("dom", "st"),
        check_vma=False,
    )
```

```python
import jax
import jax.numpy as jnp
from jax import lax
from jax.sharding import PartitionSpec as P

POLY = 3


centre = 10.0
half_span = 10.0


def ring(block, axis, step):
    count = lax.axis_size(axis)
    route = [(i, (i + step) % count) for i in range(count)]
    return lax.ppermute(block, axis, route)


def from_partner(block, axis, distance):
    count = lax.axis_size(axis)
    route = []
    for low in range(count):
        high = low | 1 << distance
        if high != low and high < count:
            route += [(low, high), (high, low)]
    return lax.ppermute(block, axis, route)


def high_low(value):
    high = lax.reduce_precision(value, exponent_bits=8, mantissa_bits=7)
    low = value - high
    return jnp.concatenate([high.astype(jnp.bfloat16), low.astype(jnp.bfloat16)], 1)


def summed_halves(both):
    width = both.shape[1] // 2
    return both[:, :width] + both[:, width:]


def body(states, inv_mass, potential, cell_matrix, connect, face_rows, rotation):
    node_count, state_count = states.shape
    cell_count, cell_size = connect.shape
    face_count = face_rows.shape[0]
    wide_count = node_count + face_count
    pad = (-cell_size) % 16
    padded_size = cell_size + pad
    cell_rows = jnp.pad(connect, ((0, 0), (0, pad)), constant_values=-1).reshape(-1)
    padded_matrix = jnp.pad(cell_matrix, ((0, pad), (0, pad)))
    wide_ids = lax.broadcasted_iota(jnp.int32, (wide_count, 1), 0)
    gather_sel = (cell_rows[:, None] == wide_ids[:, 0][None, :]).astype(jnp.bfloat16)
    scatter_sel = (wide_ids == cell_rows[None, :]).astype(jnp.bfloat16)
    rim_ids = jnp.concatenate([face_rows, wide_ids[node_count:, 0]], 0)
    rim_sel = (rim_ids[:, None] == cell_rows[None, :]).astype(jnp.bfloat16)
    face_put = (wide_ids[:node_count] == face_rows[None, :]).astype(jnp.bfloat16)
    face_take = (face_rows[:, None] == wide_ids[:node_count, 0][None, :]).astype(jnp.bfloat16)

    face_states = jnp.dot(face_take, states, preferred_element_type=jnp.float32)
    face_mass_potential = jnp.stack(
        [
            inv_mass.at[face_rows].get(mode="promise_in_bounds"),
            potential.at[face_rows].get(mode="promise_in_bounds"),
        ],
        0,
    )
    ghost_states, ghost_mass_potential = ring((face_states, face_mass_potential), "dom", -1)
    field_start = jnp.concatenate([states.astype(jnp.float32), ghost_states], 0)
    wide_mass = jnp.concatenate([inv_mass, ghost_mass_potential[0]], 0)
    wide_potential = jnp.concatenate([potential, ghost_mass_potential[1]], 0)

    def operate(field_in):
        weighted = (wide_mass[:, None] * field_in).astype(jnp.bfloat16)
        values = lax.dot_general(
            scatter_sel, weighted, (((0,), (0,)), ((), ())), preferred_element_type=jnp.float32
        )
        values = values.astype(jnp.bfloat16).reshape(cell_count, padded_size, state_count)
        products = jnp.einsum(
            "ij,cjb->cib", padded_matrix, values, preferred_element_type=jnp.float32
        ).reshape(-1, state_count)
        both = high_low(products)
        rim = summed_halves(jnp.dot(rim_sel, both, preferred_element_type=jnp.float32))
        from_prev = ring(rim[face_count:], "dom", 1)
        from_next = ring(rim[:face_count], "dom", -1)
        main = summed_halves(jnp.dot(scatter_sel, both, preferred_element_type=jnp.float32))
        own = main[:node_count] + summed_halves(
            jnp.dot(face_put, high_low(from_prev), preferred_element_type=jnp.float32)
        )
        summed = jnp.concatenate([own, main[node_count:] + from_next], 0)
        return wide_mass[:, None] * summed + wide_potential[:, None] * field_in

    def chebyshev_step(step, carry):
        previous, current = carry
        scaled = (operate(current) - centre * current) / half_span
        first = step == 0
        gain = jnp.where(first, 1.0, 2.0).astype(jnp.float32)
        keep = jnp.where(first, 0.0, 1.0).astype(jnp.float32)
        return current, gain * scaled - keep * previous

    previous, current = lax.fori_loop(0, POLY, chebyshev_step, (field_start, field_start))
    filtered = current[:node_count].astype(jnp.bfloat16)
    position = lax.axis_index("st") % 4

    def rows_for(member):
        return lax.dynamic_slice_in_dim(rotation, member * state_count, state_count, 0)

    across = from_partner(filtered, "st", 1)
    beside = from_partner(filtered, "st", 0)
    diagonal = from_partner(across, "st", 0)
    rotated = jnp.dot(filtered, rows_for(position), preferred_element_type=jnp.float32)
    rotated = rotated + jnp.dot(beside, rows_for(position ^ 1), preferred_element_type=jnp.float32)
    rotated = rotated + jnp.dot(across, rows_for(position ^ 2), preferred_element_type=jnp.float32)
    rotated = rotated + jnp.dot(
        diagonal, rows_for(position ^ 3), preferred_element_type=jnp.float32
    )
    return rotated


def solution(mesh):
    return jax.shard_map(
        body,
        mesh=mesh,
        in_specs=(P("dom", "st"), P("dom"), P("dom"), P(), P("dom", None), P("dom"), P(None, "st")),
        out_specs=P("dom", "st"),
        check_vma=False,
    )
```

```python
import jax
import jax.numpy as jnp
from jax import lax
from jax.sharding import PartitionSpec as P

POLY = 3


centre = 10.0
half_span = 10.0


def ring(block, axis, step):
    count = lax.axis_size(axis)
    route = [(i, (i + step) % count) for i in range(count)]
    return lax.ppermute(block, axis, route)


def from_partner(block, axis, distance):
    count = lax.axis_size(axis)
    route = []
    for low in range(count):
        high = low | 1 << distance
        if high != low and high < count:
            route += [(low, high), (high, low)]
    return lax.ppermute(block, axis, route)


def high_low(value):
    high = lax.reduce_precision(value, exponent_bits=8, mantissa_bits=7)
    low = value - high
    return jnp.concatenate([high.astype(jnp.bfloat16), low.astype(jnp.bfloat16)], 1)


def summed_halves(both):
    width = both.shape[1] // 2
    return both[:, :width] + both[:, width:]


def body(states, inv_mass, potential, cell_matrix, connect, face_rows, rotation):
    node_count, state_count = states.shape
    cell_count, cell_size = connect.shape
    face_count = face_rows.shape[0]
    wide_count = node_count + face_count
    pad = (-cell_size) % 128
    padded_size = cell_size + pad
    cell_rows = jnp.pad(connect, ((0, 0), (0, pad)), constant_values=-1).reshape(-1)
    padded_matrix = jnp.pad(cell_matrix, ((0, pad), (0, pad)))
    wide_ids = lax.broadcasted_iota(jnp.int32, (wide_count, 1), 0)
    gather_sel = (cell_rows[:, None] == wide_ids[:, 0][None, :]).astype(jnp.bfloat16)
    scatter_sel = (wide_ids == cell_rows[None, :]).astype(jnp.bfloat16)
    rim_ids = jnp.concatenate([face_rows, wide_ids[node_count:, 0]], 0)
    rim_sel = (rim_ids[:, None] == cell_rows[None, :]).astype(jnp.bfloat16)
    face_put = (wide_ids[:node_count] == face_rows[None, :]).astype(jnp.bfloat16)
    face_take = (face_rows[:, None] == wide_ids[:node_count, 0][None, :]).astype(jnp.bfloat16)

    face_states = jnp.dot(face_take, states, preferred_element_type=jnp.float32)
    face_mass_potential = lax.dot_general(
        jnp.stack([inv_mass, potential], 0),
        face_put.astype(jnp.float32),
        (((1,), (0,)), ((), ())),
        precision=lax.Precision.HIGHEST,
        preferred_element_type=jnp.float32,
    )
    ghost_states, ghost_mass_potential = ring((face_states, face_mass_potential), "dom", -1)
    field_start = jnp.concatenate([states.astype(jnp.float32), ghost_states], 0)
    wide_mass = jnp.concatenate([inv_mass, ghost_mass_potential[0]], 0)
    wide_potential = jnp.concatenate([potential, ghost_mass_potential[1]], 0)

    def operate(field_in):
        weighted = (wide_mass[:, None] * field_in).astype(jnp.bfloat16)
        values = lax.dot_general(
            scatter_sel, weighted, (((0,), (0,)), ((), ())), preferred_element_type=jnp.float32
        )
        values = values.astype(jnp.bfloat16).reshape(cell_count, padded_size, state_count)
        products = jnp.einsum(
            "ij,cjb->cib", padded_matrix, values, preferred_element_type=jnp.float32
        ).reshape(-1, state_count)
        both = high_low(products)
        rim = summed_halves(jnp.dot(rim_sel, both, preferred_element_type=jnp.float32))
        from_prev = ring(rim[face_count:], "dom", 1)
        from_next = ring(rim[:face_count], "dom", -1)
        main = summed_halves(jnp.dot(scatter_sel, both, preferred_element_type=jnp.float32))
        own = main[:node_count] + summed_halves(
            jnp.dot(face_put, high_low(from_prev), preferred_element_type=jnp.float32)
        )
        summed = jnp.concatenate([own, main[node_count:] + from_next], 0)
        return wide_mass[:, None] * summed + wide_potential[:, None] * field_in

    def chebyshev_step(step, carry):
        previous, current = carry
        scaled = (operate(current) - centre * current) / half_span
        first = step == 0
        gain = jnp.where(first, 1.0, 2.0).astype(jnp.float32)
        keep = jnp.where(first, 0.0, 1.0).astype(jnp.float32)
        return current, gain * scaled - keep * previous

    previous, current = lax.fori_loop(0, POLY, chebyshev_step, (field_start, field_start))
    filtered = current[:node_count].astype(jnp.bfloat16)
    position = lax.axis_index("st") % 4

    def rows_for(member):
        return lax.dynamic_slice_in_dim(rotation, member * state_count, state_count, 0)

    across = from_partner(filtered, "st", 1)
    beside = from_partner(filtered, "st", 0)
    diagonal = from_partner(across, "st", 0)
    rotated = jnp.dot(filtered, rows_for(position), preferred_element_type=jnp.float32)
    rotated = rotated + jnp.dot(beside, rows_for(position ^ 1), preferred_element_type=jnp.float32)
    rotated = rotated + jnp.dot(across, rows_for(position ^ 2), preferred_element_type=jnp.float32)
    rotated = rotated + jnp.dot(
        diagonal, rows_for(position ^ 3), preferred_element_type=jnp.float32
    )
    return rotated


def solution(mesh):
    return jax.shard_map(
        body,
        mesh=mesh,
        in_specs=(P("dom", "st"), P("dom"), P("dom"), P(), P("dom", None), P("dom"), P(None, "st")),
        out_specs=P("dom", "st"),
        check_vma=False,
    )
```

```python
import jax
import jax.numpy as jnp
from jax import lax
from jax.sharding import PartitionSpec as P

POLY = 3


centre = 10.0
half_span = 10.0


def ring(block, axis, step):
    count = lax.axis_size(axis)
    route = [(i, (i + step) % count) for i in range(count)]
    return lax.ppermute(block, axis, route)


def from_partner(block, axis, distance):
    count = lax.axis_size(axis)
    route = []
    for low in range(count):
        high = low | 1 << distance
        if high != low and high < count:
            route += [(low, high), (high, low)]
    return lax.ppermute(block, axis, route)


def high_low(value):
    high = lax.reduce_precision(value, exponent_bits=8, mantissa_bits=7)
    low = value - high
    return jnp.concatenate([high.astype(jnp.bfloat16), low.astype(jnp.bfloat16)], 1)


def summed_halves(both):
    width = both.shape[1] // 2
    return both[:, :width] + both[:, width:]


def body(states, inv_mass, potential, cell_matrix, connect, face_rows, rotation):
    node_count, state_count = states.shape
    cell_count, cell_size = connect.shape
    face_count = face_rows.shape[0]
    wide_count = node_count + face_count
    pad = (-cell_size) % 16
    padded_size = cell_size + pad
    cell_rows = jnp.pad(connect, ((0, 0), (0, pad)), constant_values=-1).reshape(-1)
    padded_matrix = jnp.pad(cell_matrix, ((0, pad), (0, pad)))
    wide_ids = lax.broadcasted_iota(jnp.int32, (wide_count, 1), 0)
    gather_sel = (cell_rows[:, None] == wide_ids[:, 0][None, :]).astype(jnp.bfloat16)
    scatter_sel = (wide_ids == cell_rows[None, :]).astype(jnp.bfloat16)
    rim_ids = jnp.concatenate([face_rows, wide_ids[node_count:, 0]], 0)
    rim_sel = (rim_ids[:, None] == cell_rows[None, :]).astype(jnp.bfloat16)
    face_put = (wide_ids[:node_count] == face_rows[None, :]).astype(jnp.bfloat16)
    face_take = (face_rows[:, None] == wide_ids[:node_count, 0][None, :]).astype(jnp.bfloat16)

    face_states = jnp.dot(face_take, states, preferred_element_type=jnp.float32)
    face_mass_potential = lax.dot_general(
        jnp.stack([inv_mass, potential], 0),
        face_put.astype(jnp.float32),
        (((1,), (0,)), ((), ())),
        precision=lax.Precision.HIGHEST,
        preferred_element_type=jnp.float32,
    )
    ghost_states, ghost_mass_potential = ring((face_states, face_mass_potential), "dom", -1)
    field_start = jnp.concatenate([states.astype(jnp.float32), ghost_states], 0)
    wide_mass = jnp.concatenate([inv_mass, ghost_mass_potential[0]], 0)
    wide_potential = jnp.concatenate([potential, ghost_mass_potential[1]], 0)

    def operate(field_in):
        weighted = (wide_mass[:, None] * field_in).astype(jnp.bfloat16)
        values = lax.dot_general(
            scatter_sel, weighted, (((0,), (0,)), ((), ())), preferred_element_type=jnp.float32
        )
        values = values.astype(jnp.bfloat16).reshape(cell_count, padded_size, state_count)
        products = jnp.einsum(
            "ij,cjb->cib", padded_matrix, values, preferred_element_type=jnp.float32
        ).reshape(-1, state_count)
        both = high_low(products)
        rim = summed_halves(jnp.dot(rim_sel, both, preferred_element_type=jnp.float32))
        from_prev = ring(rim[face_count:], "dom", 1)
        from_next = ring(rim[:face_count], "dom", -1)
        main = summed_halves(jnp.dot(scatter_sel, both, preferred_element_type=jnp.float32))
        own = main[:node_count] + summed_halves(
            jnp.dot(face_put, high_low(from_prev), preferred_element_type=jnp.float32)
        )
        summed = jnp.concatenate([own, main[node_count:] + from_next], 0)
        return wide_mass[:, None] * summed + wide_potential[:, None] * field_in

    def chebyshev_step(step, carry):
        previous, current = carry
        scaled = (operate(current) - centre * current) / half_span
        first = step == 0
        gain = jnp.where(first, 1.0, 2.0).astype(jnp.float32)
        keep = jnp.where(first, 0.0, 1.0).astype(jnp.float32)
        return current, gain * scaled - keep * previous

    previous, current = lax.fori_loop(0, POLY, chebyshev_step, (field_start, field_start))
    filtered = current[:node_count].astype(jnp.bfloat16)
    position = lax.axis_index("st") % 4

    def rows_for(member):
        return lax.dynamic_slice_in_dim(rotation, member * state_count, state_count, 0)

    halves = 2 if node_count % 32 == 0 else 1
    half = node_count // halves
    parts = [filtered[part * half : (part + 1) * half] for part in range(halves)]
    across = [from_partner(part, "st", 1) for part in parts]
    beside = from_partner(filtered, "st", 0)
    diagonal = jnp.concatenate([from_partner(piece, "st", 0) for piece in across], 0)
    across = jnp.concatenate(across, 0)
    rotated = jnp.dot(filtered, rows_for(position), preferred_element_type=jnp.float32)
    rotated = rotated + jnp.dot(beside, rows_for(position ^ 1), preferred_element_type=jnp.float32)
    rotated = rotated + jnp.dot(across, rows_for(position ^ 2), preferred_element_type=jnp.float32)
    rotated = rotated + jnp.dot(
        diagonal, rows_for(position ^ 3), preferred_element_type=jnp.float32
    )
    return rotated


def solution(mesh):
    return jax.shard_map(
        body,
        mesh=mesh,
        in_specs=(P("dom", "st"), P("dom"), P("dom"), P(), P("dom", None), P("dom"), P(None, "st")),
        out_specs=P("dom", "st"),
        check_vma=False,
    )
```

```python
import jax
import jax.numpy as jnp
from jax import lax
from jax.sharding import PartitionSpec as P

POLY = 3


centre = 10.0
half_span = 10.0


def ring(block, axis, step):
    count = lax.axis_size(axis)
    route = [(i, (i + step) % count) for i in range(count)]
    return lax.ppermute(block, axis, route)


def from_partner(block, axis, distance):
    count = lax.axis_size(axis)
    route = []
    for low in range(count):
        high = low | 1 << distance
        if high != low and high < count:
            route += [(low, high), (high, low)]
    return lax.ppermute(block, axis, route)


def high_low(value):
    high = lax.reduce_precision(value, exponent_bits=8, mantissa_bits=7)
    low = value - high
    return jnp.concatenate([high.astype(jnp.bfloat16), low.astype(jnp.bfloat16)], 1)


def summed_halves(both):
    width = both.shape[1] // 2
    return both[:, :width] + both[:, width:]


def body(states, inv_mass, potential, cell_matrix, connect, face_rows, rotation):
    node_count, state_count = states.shape
    cell_count, cell_size = connect.shape
    face_count = face_rows.shape[0]
    wide_count = node_count + face_count
    pad = (-cell_size) % 16
    padded_size = cell_size + pad
    cell_rows = jnp.pad(connect, ((0, 0), (0, pad)), constant_values=-1).reshape(-1)
    padded_matrix = jnp.pad(cell_matrix, ((0, pad), (0, pad)))
    wide_ids = lax.broadcasted_iota(jnp.int32, (wide_count, 1), 0)
    gather_sel = (cell_rows[:, None] == wide_ids[:, 0][None, :]).astype(jnp.bfloat16)
    scatter_sel = (wide_ids == cell_rows[None, :]).astype(jnp.bfloat16)
    rim_ids = jnp.concatenate([face_rows, wide_ids[node_count:, 0]], 0)
    rim_sel = (rim_ids[:, None] == cell_rows[None, :]).astype(jnp.bfloat16)
    face_put = (wide_ids[:node_count] == face_rows[None, :]).astype(jnp.bfloat16)
    face_take = (face_rows[:, None] == wide_ids[:node_count, 0][None, :]).astype(jnp.bfloat16)

    face_states = jnp.dot(face_take, states, preferred_element_type=jnp.float32)
    face_mass_potential = lax.dot_general(
        face_put.astype(jnp.float32),
        jnp.stack([inv_mass, potential], 0),
        (((0,), (1,)), ((), ())),
        precision=lax.Precision.HIGHEST,
        preferred_element_type=jnp.float32,
    )
    ghost = ring(jnp.concatenate([face_states, face_mass_potential], 1), "dom", -1)
    field_start = jnp.concatenate([states.astype(jnp.float32), ghost[:, :state_count]], 0)
    wide_mass = jnp.concatenate([inv_mass, ghost[:, state_count]], 0)
    wide_potential = jnp.concatenate([potential, ghost[:, state_count + 1]], 0)

    def operate(field_in):
        weighted = (wide_mass[:, None] * field_in).astype(jnp.bfloat16)
        values = lax.dot_general(
            scatter_sel, weighted, (((0,), (0,)), ((), ())), preferred_element_type=jnp.float32
        )
        values = values.astype(jnp.bfloat16).reshape(cell_count, padded_size, state_count)
        products = jnp.einsum(
            "ij,cjb->cib", padded_matrix, values, preferred_element_type=jnp.float32
        ).reshape(-1, state_count)
        both = high_low(products)
        rim = summed_halves(jnp.dot(rim_sel, both, preferred_element_type=jnp.float32))
        from_prev = ring(rim[face_count:], "dom", 1)
        from_next = ring(rim[:face_count], "dom", -1)
        main = summed_halves(jnp.dot(scatter_sel, both, preferred_element_type=jnp.float32))
        own = main[:node_count] + summed_halves(
            jnp.dot(face_put, high_low(from_prev), preferred_element_type=jnp.float32)
        )
        summed = jnp.concatenate([own, main[node_count:] + from_next], 0)
        return wide_mass[:, None] * summed + wide_potential[:, None] * field_in

    def chebyshev_step(step, carry):
        previous, current = carry
        scaled = (operate(current) - centre * current) / half_span
        first = step == 0
        gain = jnp.where(first, 1.0, 2.0).astype(jnp.float32)
        keep = jnp.where(first, 0.0, 1.0).astype(jnp.float32)
        return current, gain * scaled - keep * previous

    previous, current = lax.fori_loop(0, POLY, chebyshev_step, (field_start, field_start))
    filtered = current[:node_count].astype(jnp.bfloat16)
    position = lax.axis_index("st") % 4

    def rows_for(member):
        return lax.dynamic_slice_in_dim(rotation, member * state_count, state_count, 0)

    across = from_partner(filtered, "st", 1)
    beside = from_partner(filtered, "st", 0)
    diagonal = from_partner(across, "st", 0)
    rotated = jnp.dot(filtered, rows_for(position), preferred_element_type=jnp.float32)
    rotated = rotated + jnp.dot(beside, rows_for(position ^ 1), preferred_element_type=jnp.float32)
    rotated = rotated + jnp.dot(across, rows_for(position ^ 2), preferred_element_type=jnp.float32)
    rotated = rotated + jnp.dot(
        diagonal, rows_for(position ^ 3), preferred_element_type=jnp.float32
    )
    return rotated


def solution(mesh):
    return jax.shard_map(
        body,
        mesh=mesh,
        in_specs=(P("dom", "st"), P("dom"), P("dom"), P(), P("dom", None), P("dom"), P(None, "st")),
        out_specs=P("dom", "st"),
        check_vma=False,
    )
```

```python
import jax
import jax.numpy as jnp
from jax import lax
from jax.sharding import PartitionSpec as P

POLY = 3


centre = 10.0
half_span = 10.0


def ring(block, axis, step):
    count = lax.axis_size(axis)
    route = [(i, (i + step) % count) for i in range(count)]
    return lax.ppermute(block, axis, route)


def from_partner(block, axis, distance):
    count = lax.axis_size(axis)
    route = []
    for low in range(count):
        high = low | 1 << distance
        if high != low and high < count:
            route += [(low, high), (high, low)]
    return lax.ppermute(block, axis, route)


def high_low(value):
    high = lax.reduce_precision(value, exponent_bits=8, mantissa_bits=7)
    low = value - high
    return jnp.concatenate([high.astype(jnp.bfloat16), low.astype(jnp.bfloat16)], 1)


def summed_halves(both):
    width = both.shape[1] // 2
    return both[:, :width] + both[:, width:]


def body(states, inv_mass, potential, cell_matrix, connect, face_rows, rotation):
    node_count, state_count = states.shape
    cell_count, cell_size = connect.shape
    face_count = face_rows.shape[0]
    wide_count = node_count + face_count
    pad = (-cell_size) % 16
    padded_size = cell_size + pad
    cell_rows = jnp.pad(connect, ((0, 0), (0, pad)), constant_values=-1).reshape(-1)
    padded_matrix = jnp.pad(cell_matrix, ((0, pad), (0, pad)))
    wide_ids = lax.broadcasted_iota(jnp.int32, (wide_count, 1), 0)
    gather_sel = (cell_rows[:, None] == wide_ids[:, 0][None, :]).astype(jnp.bfloat16)
    scatter_sel = (wide_ids == cell_rows[None, :]).astype(jnp.bfloat16)
    rim_ids = jnp.concatenate([face_rows, wide_ids[node_count:, 0]], 0)
    rim_sel = (rim_ids[:, None] == cell_rows[None, :]).astype(jnp.bfloat16)
    face_put = (wide_ids[:node_count] == face_rows[None, :]).astype(jnp.bfloat16)
    face_take = (face_rows[:, None] == wide_ids[:node_count, 0][None, :]).astype(jnp.bfloat16)

    face_states = jnp.dot(face_take, states, preferred_element_type=jnp.float32)
    face_mass_potential = lax.dot_general(
        jnp.stack([inv_mass, potential], 0),
        face_put.astype(jnp.float32),
        (((1,), (0,)), ((), ())),
        precision=lax.Precision.HIGHEST,
        preferred_element_type=jnp.float32,
    )
    ghost_states, ghost_mass_potential = ring((face_states, face_mass_potential), "dom", -1)
    field_start = jnp.concatenate([states.astype(jnp.float32), ghost_states], 0)
    wide_mass = jnp.concatenate([inv_mass, ghost_mass_potential[0]], 0)
    wide_potential = jnp.concatenate([potential, ghost_mass_potential[1]], 0)

    def operate(field_in):
        weighted = (wide_mass[:, None] * field_in).astype(jnp.bfloat16)
        values = lax.dot_general(
            scatter_sel, weighted, (((0,), (0,)), ((), ())), preferred_element_type=jnp.float32
        )
        values = values.astype(jnp.bfloat16).reshape(cell_count, padded_size, state_count)
        products = jnp.einsum(
            "ij,cjb->cib", padded_matrix, values, preferred_element_type=jnp.float32
        ).reshape(-1, state_count)
        both = high_low(products)
        rim = summed_halves(jnp.dot(rim_sel, both, preferred_element_type=jnp.float32))
        from_prev = ring(rim[face_count:], "dom", 1)
        from_next = ring(rim[:face_count], "dom", -1)
        main = summed_halves(jnp.dot(scatter_sel, both, preferred_element_type=jnp.float32))
        base = lax.optimization_barrier(
            wide_mass[:node_count, None] * main[:node_count]
            + wide_potential[:node_count, None] * field_in[:node_count]
        )
        face_add = summed_halves(
            jnp.dot(face_put, high_low(from_prev), preferred_element_type=jnp.float32)
        )
        own = base + wide_mass[:node_count, None] * face_add
        ghost_rows = slice(node_count, None)
        ghost = wide_mass[ghost_rows, None] * (main[ghost_rows] + from_next) + wide_potential[
            ghost_rows, None
        ] * field_in[ghost_rows]
        return jnp.concatenate([own, ghost], 0)

    def chebyshev_step(step, carry):
        previous, current = carry
        scaled = (operate(current) - centre * current) / half_span
        first = step == 0
        gain = jnp.where(first, 1.0, 2.0).astype(jnp.float32)
        keep = jnp.where(first, 0.0, 1.0).astype(jnp.float32)
        return current, gain * scaled - keep * previous

    previous, current = lax.fori_loop(0, POLY, chebyshev_step, (field_start, field_start))
    filtered = current[:node_count].astype(jnp.bfloat16)
    position = lax.axis_index("st") % 4

    def rows_for(member):
        return lax.dynamic_slice_in_dim(rotation, member * state_count, state_count, 0)

    across = from_partner(filtered, "st", 1)
    beside = from_partner(filtered, "st", 0)
    diagonal = from_partner(across, "st", 0)
    rotated = jnp.dot(filtered, rows_for(position), preferred_element_type=jnp.float32)
    rotated = rotated + jnp.dot(beside, rows_for(position ^ 1), preferred_element_type=jnp.float32)
    rotated = rotated + jnp.dot(across, rows_for(position ^ 2), preferred_element_type=jnp.float32)
    rotated = rotated + jnp.dot(
        diagonal, rows_for(position ^ 3), preferred_element_type=jnp.float32
    )
    return rotated


def solution(mesh):
    return jax.shard_map(
        body,
        mesh=mesh,
        in_specs=(P("dom", "st"), P("dom"), P("dom"), P(), P("dom", None), P("dom"), P(None, "st")),
        out_specs=P("dom", "st"),
        check_vma=False,
    )
```

```python
import jax
import jax.numpy as jnp
from jax import lax
from jax.sharding import PartitionSpec as P

POLY = 3


centre = 10.0
half_span = 10.0


def ring(block, axis, step):
    count = lax.axis_size(axis)
    route = [(i, (i + step) % count) for i in range(count)]
    return lax.ppermute(block, axis, route)


def from_partner(block, axis, distance):
    count = lax.axis_size(axis)
    route = []
    for low in range(count):
        high = low | 1 << distance
        if high != low and high < count:
            route += [(low, high), (high, low)]
    return lax.ppermute(block, axis, route)


def high_low(value):
    high = lax.reduce_precision(value, exponent_bits=8, mantissa_bits=7)
    low = value - high
    return jnp.concatenate([high.astype(jnp.bfloat16), low.astype(jnp.bfloat16)], 1)


def summed_halves(both):
    width = both.shape[1] // 2
    return both[:, :width] + both[:, width:]


def body(states, inv_mass, potential, cell_matrix, connect, face_rows, rotation):
    node_count, state_count = states.shape
    cell_count, cell_size = connect.shape
    face_count = face_rows.shape[0]
    wide_count = node_count + face_count
    pad = (-cell_size) % 16
    padded_size = cell_size + pad
    cell_rows = jnp.pad(connect, ((0, 0), (0, pad)), constant_values=-1).reshape(-1)
    padded_matrix = jnp.pad(cell_matrix, ((0, pad), (0, pad)))
    wide_ids = lax.broadcasted_iota(jnp.int32, (wide_count, 1), 0)
    gather_sel = (cell_rows[:, None] == wide_ids[:, 0][None, :]).astype(jnp.bfloat16)
    scatter_sel = (wide_ids == cell_rows[None, :]).astype(jnp.bfloat16)
    rim_ids = jnp.concatenate([face_rows, wide_ids[node_count:, 0]], 0)
    rim_sel = (rim_ids[:, None] == cell_rows[None, :]).astype(jnp.bfloat16)
    face_put = (wide_ids[:node_count] == face_rows[None, :]).astype(jnp.bfloat16)
    face_take = (face_rows[:, None] == wide_ids[:node_count, 0][None, :]).astype(jnp.bfloat16)

    face_states = jnp.dot(face_take, states, preferred_element_type=jnp.float32)
    face_mass_potential = lax.dot_general(
        jnp.stack([inv_mass, potential], 0),
        face_put.astype(jnp.float32),
        (((1,), (0,)), ((), ())),
        precision=lax.Precision.HIGHEST,
        preferred_element_type=jnp.float32,
    )
    ghost_states, ghost_mass_potential = ring((face_states, face_mass_potential), "dom", -1)
    field_start = jnp.concatenate([states.astype(jnp.float32), ghost_states], 0)
    wide_mass = jnp.concatenate([inv_mass, ghost_mass_potential[0]], 0)
    wide_potential = jnp.concatenate([potential, ghost_mass_potential[1]], 0)

    def operate(field_in):
        weighted = (wide_mass[:, None] * field_in).astype(jnp.bfloat16)
        values = lax.dot_general(
            scatter_sel, weighted, (((0,), (0,)), ((), ())), preferred_element_type=jnp.float32
        )
        values = values.astype(jnp.bfloat16).reshape(cell_count, padded_size, state_count)
        products = jnp.einsum(
            "ij,cjb->cib", padded_matrix, values, preferred_element_type=jnp.float32
        ).reshape(-1, state_count)
        both = high_low(products)
        rim = summed_halves(jnp.dot(rim_sel, both, preferred_element_type=jnp.float32))
        from_prev = ring(rim[face_count:], "dom", 1)
        from_next = ring(rim[:face_count], "dom", -1)
        main = summed_halves(jnp.dot(scatter_sel, both, preferred_element_type=jnp.float32))
        own = main[:node_count] + summed_halves(
            jnp.dot(face_put, high_low(from_prev), preferred_element_type=jnp.float32)
        )
        summed = jnp.concatenate([own, main[node_count:] + from_next], 0)
        return wide_mass[:, None] * summed + wide_potential[:, None] * field_in

    def chebyshev_step(step, carry):
        previous, current = carry
        scaled = (operate(current) - centre * current) / half_span
        first = step == 0
        gain = jnp.where(first, 1.0, 2.0).astype(jnp.float32)
        keep = jnp.where(first, 0.0, 1.0).astype(jnp.float32)
        return current, gain * scaled - keep * previous

    previous, current = lax.fori_loop(0, POLY, chebyshev_step, (field_start, field_start))
    filtered = current[:node_count].astype(jnp.bfloat16)
    position = lax.axis_index("st") % 4

    def rows_for(member):
        return lax.dynamic_slice_in_dim(rotation, member * state_count, state_count, 0)

    across = from_partner(filtered, "st", 1)
    beside = from_partner(filtered, "st", 0)
    diagonal = from_partner(across, "st", 0)
    blocks = jnp.concatenate([filtered, beside, across, diagonal], 1)
    turn = jnp.concatenate([rows_for(position ^ member) for member in range(4)], 0)
    rotated = jnp.dot(blocks, turn, preferred_element_type=jnp.float32)
    return rotated


def solution(mesh):
    return jax.shard_map(
        body,
        mesh=mesh,
        in_specs=(P("dom", "st"), P("dom"), P("dom"), P(), P("dom", None), P("dom"), P(None, "st")),
        out_specs=P("dom", "st"),
        check_vma=False,
    )
```

```python
import jax
import jax.numpy as jnp
from jax import lax
from jax.sharding import PartitionSpec as P

POLY = 3


centre = 10.0
half_span = 10.0


def ring(block, axis, step):
    count = lax.axis_size(axis)
    route = [(i, (i + step) % count) for i in range(count)]
    return lax.ppermute(block, axis, route)


def from_partner(block, axis, distance):
    count = lax.axis_size(axis)
    route = []
    for low in range(count):
        high = low | 1 << distance
        if high != low and high < count:
            route += [(low, high), (high, low)]
    return lax.ppermute(block, axis, route)


def high_low(value):
    high = lax.reduce_precision(value, exponent_bits=8, mantissa_bits=7)
    low = value - high
    return jnp.concatenate([high.astype(jnp.bfloat16), low.astype(jnp.bfloat16)], 1)


def summed_halves(both):
    width = both.shape[1] // 2
    return both[:, :width] + both[:, width:]


def body(states, inv_mass, potential, cell_matrix, connect, face_rows, rotation):
    node_count, state_count = states.shape
    cell_count, cell_size = connect.shape
    face_count = face_rows.shape[0]
    wide_count = node_count + face_count
    pad = (-cell_size) % 16
    padded_size = cell_size + pad
    cell_rows = jnp.pad(connect, ((0, 0), (0, pad)), constant_values=-1).reshape(-1)
    padded_matrix = jnp.pad(cell_matrix, ((0, pad), (0, pad)))
    wide_ids = lax.broadcasted_iota(jnp.int32, (wide_count, 1), 0)
    gather_sel = (cell_rows[:, None] == wide_ids[:, 0][None, :]).astype(jnp.bfloat16)
    scatter_sel = (wide_ids == cell_rows[None, :]).astype(jnp.bfloat16)
    rim_ids = jnp.concatenate([face_rows, wide_ids[node_count:, 0]], 0)
    rim_sel = (rim_ids[:, None] == cell_rows[None, :]).astype(jnp.bfloat16)
    face_put = (wide_ids[:node_count] == face_rows[None, :]).astype(jnp.bfloat16)
    face_take = (face_rows[:, None] == wide_ids[:node_count, 0][None, :]).astype(jnp.bfloat16)

    face_states = jnp.dot(face_take, states, preferred_element_type=jnp.float32)
    face_mass_potential = lax.dot_general(
        jnp.stack([inv_mass, potential], 0),
        face_put.astype(jnp.float32),
        (((1,), (0,)), ((), ())),
        precision=lax.Precision.HIGHEST,
        preferred_element_type=jnp.float32,
    )
    ghost_states, ghost_mass_potential = ring((face_states, face_mass_potential), "dom", -1)
    field_start = jnp.concatenate([states.astype(jnp.float32), ghost_states], 0)
    wide_mass = jnp.concatenate([inv_mass, ghost_mass_potential[0]], 0)
    wide_potential = jnp.concatenate([potential, ghost_mass_potential[1]], 0)

    def operate(field_in):
        weighted = (wide_mass[:, None] * field_in).astype(jnp.bfloat16)
        values = lax.dot_general(
            scatter_sel, weighted, (((0,), (0,)), ((), ())), preferred_element_type=jnp.float32
        )
        values = values.astype(jnp.bfloat16).reshape(cell_count, padded_size, state_count)
        products = jnp.einsum(
            "ij,cjb->cib", padded_matrix, values, preferred_element_type=jnp.float32
        ).reshape(-1, state_count)
        both = high_low(products)
        rim = summed_halves(jnp.dot(rim_sel, both, preferred_element_type=jnp.float32))
        from_prev = ring(high_low(rim[face_count:]), "dom", 1)
        from_next = ring(rim[:face_count], "dom", -1)
        main = summed_halves(jnp.dot(scatter_sel, both, preferred_element_type=jnp.float32))
        own = main[:node_count] + summed_halves(
            jnp.dot(face_put, from_prev, preferred_element_type=jnp.float32)
        )
        summed = jnp.concatenate([own, main[node_count:] + from_next], 0)
        return wide_mass[:, None] * summed + wide_potential[:, None] * field_in

    def chebyshev_step(step, carry):
        previous, current = carry
        scaled = (operate(current) - centre * current) / half_span
        first = step == 0
        gain = jnp.where(first, 1.0, 2.0).astype(jnp.float32)
        keep = jnp.where(first, 0.0, 1.0).astype(jnp.float32)
        return current, gain * scaled - keep * previous

    previous, current = lax.fori_loop(0, POLY, chebyshev_step, (field_start, field_start))
    filtered = current[:node_count].astype(jnp.bfloat16)
    position = lax.axis_index("st") % 4

    def rows_for(member):
        return lax.dynamic_slice_in_dim(rotation, member * state_count, state_count, 0)

    across = from_partner(filtered, "st", 1)
    beside = from_partner(filtered, "st", 0)
    diagonal = from_partner(across, "st", 0)
    rotated = jnp.dot(filtered, rows_for(position), preferred_element_type=jnp.float32)
    rotated = rotated + jnp.dot(beside, rows_for(position ^ 1), preferred_element_type=jnp.float32)
    rotated = rotated + jnp.dot(across, rows_for(position ^ 2), preferred_element_type=jnp.float32)
    rotated = rotated + jnp.dot(
        diagonal, rows_for(position ^ 3), preferred_element_type=jnp.float32
    )
    return rotated


def solution(mesh):
    return jax.shard_map(
        body,
        mesh=mesh,
        in_specs=(P("dom", "st"), P("dom"), P("dom"), P(), P("dom", None), P("dom"), P(None, "st")),
        out_specs=P("dom", "st"),
        check_vma=False,
    )
```

```python
import jax
import jax.numpy as jnp
from jax import lax
from jax.sharding import PartitionSpec as P

POLY = 3


centre = 10.0
half_span = 10.0


def ring(block, axis, step):
    count = lax.axis_size(axis)
    route = [(i, (i + step) % count) for i in range(count)]
    return lax.ppermute(block, axis, route)


def from_partner(block, axis, distance):
    count = lax.axis_size(axis)
    route = []
    for low in range(count):
        high = low | 1 << distance
        if high != low and high < count:
            route += [(low, high), (high, low)]
    return lax.ppermute(block, axis, route)


def high_low(value):
    high = lax.reduce_precision(value, exponent_bits=8, mantissa_bits=7)
    low = value - high
    return jnp.concatenate([high.astype(jnp.bfloat16), low.astype(jnp.bfloat16)], 1)


def summed_halves(both):
    width = both.shape[1] // 2
    return both[:, :width] + both[:, width:]


def body(states, inv_mass, potential, cell_matrix, connect, face_rows, rotation):
    node_count, state_count = states.shape
    cell_count, cell_size = connect.shape
    face_count = face_rows.shape[0]
    wide_count = node_count + face_count
    pad = (-cell_size) % 16
    padded_size = cell_size + pad
    cell_rows = jnp.pad(connect, ((0, 0), (0, pad)), constant_values=-1).reshape(-1)
    padded_matrix = jnp.pad(cell_matrix, ((0, pad), (0, pad)))
    wide_ids = lax.broadcasted_iota(jnp.int32, (wide_count, 1), 0)
    gather_sel = (cell_rows[:, None] == wide_ids[:, 0][None, :]).astype(jnp.bfloat16)
    scatter_sel = (wide_ids == cell_rows[None, :]).astype(jnp.bfloat16)
    rim_ids = jnp.concatenate([face_rows, wide_ids[node_count:, 0]], 0)
    rim_sel = (rim_ids[:, None] == cell_rows[None, :]).astype(jnp.bfloat16)
    face_put = (wide_ids[:node_count] == face_rows[None, :]).astype(jnp.bfloat16)
    face_take = (face_rows[:, None] == wide_ids[:node_count, 0][None, :]).astype(jnp.bfloat16)

    face_states = jnp.dot(face_take, states, preferred_element_type=jnp.float32)
    face_mass_potential = lax.dot_general(
        jnp.stack([inv_mass, potential], 0),
        face_put.astype(jnp.float32),
        (((1,), (0,)), ((), ())),
        precision=lax.Precision.HIGHEST,
        preferred_element_type=jnp.float32,
    )
    ghost_states, ghost_mass_potential = ring((face_states, face_mass_potential), "dom", -1)
    field_start = jnp.concatenate([states.astype(jnp.float32), ghost_states], 0)
    wide_mass = jnp.concatenate([inv_mass, ghost_mass_potential[0]], 0)
    wide_potential = jnp.concatenate([potential, ghost_mass_potential[1]], 0)

    def operate(field_in):
        weighted = (wide_mass[:, None] * field_in).astype(jnp.bfloat16)
        values = lax.dot_general(
            scatter_sel, weighted, (((0,), (0,)), ((), ())), preferred_element_type=jnp.float32
        )
        values = values.astype(jnp.bfloat16).reshape(cell_count, padded_size, state_count)
        products = jnp.einsum(
            "ij,cjb->cib", padded_matrix, values, preferred_element_type=jnp.float32
        ).reshape(-1, state_count)
        both = high_low(products)
        rim = summed_halves(jnp.dot(rim_sel, both, preferred_element_type=jnp.float32))
        from_prev = ring(rim[face_count:], "dom", 1)
        from_next = ring(rim[:face_count], "dom", -1)
        main = summed_halves(jnp.dot(scatter_sel, both, preferred_element_type=jnp.float32))
        own = main[:node_count] + summed_halves(
            jnp.dot(face_put, high_low(from_prev), preferred_element_type=jnp.float32)
        )
        summed = jnp.concatenate([own, main[node_count:] + from_next], 0)
        return wide_mass[:, None] * summed + wide_potential[:, None] * field_in

    def chebyshev_step(step, carry):
        previous, current = carry
        scaled = (operate(current) - centre * current) / half_span
        first = step == 0
        gain = jnp.where(first, 1.0, 2.0).astype(jnp.float32)
        keep = jnp.where(first, 0.0, 1.0).astype(jnp.float32)
        return current, gain * scaled - keep * previous

    previous, current = lax.fori_loop(
        0, POLY - 1, chebyshev_step, (field_start, field_start)
    )

    weighted = (wide_mass[:, None] * current).astype(jnp.bfloat16)
    values = lax.dot_general(
        scatter_sel, weighted, (((0,), (0,)), ((), ())), preferred_element_type=jnp.float32
    )
    values = values.astype(jnp.bfloat16).reshape(cell_count, padded_size, state_count)
    products = jnp.einsum(
        "ij,cjb->cib", padded_matrix, values, preferred_element_type=jnp.float32
    ).reshape(-1, state_count)
    both = high_low(products)
    ghost_part = summed_halves(
        jnp.dot(rim_sel[face_count:], both, preferred_element_type=jnp.float32)
    )
    from_prev = ring(ghost_part, "dom", 1)
    main = summed_halves(
        jnp.dot(scatter_sel[:node_count], both, preferred_element_type=jnp.float32)
    )
    own = main + summed_halves(
        jnp.dot(face_put, high_low(from_prev), preferred_element_type=jnp.float32)
    )
    field = current[:node_count]
    applied = wide_mass[:node_count, None] * own + wide_potential[:node_count, None] * field
    scaled = (applied - centre * field) / half_span
    current = 2.0 * scaled - previous[:node_count]
    filtered = current[:node_count].astype(jnp.bfloat16)
    position = lax.axis_index("st") % 4

    def rows_for(member):
        return lax.dynamic_slice_in_dim(rotation, member * state_count, state_count, 0)

    across = from_partner(filtered, "st", 1)
    beside = from_partner(filtered, "st", 0)
    diagonal = from_partner(across, "st", 0)
    rotated = jnp.dot(filtered, rows_for(position), preferred_element_type=jnp.float32)
    rotated = rotated + jnp.dot(beside, rows_for(position ^ 1), preferred_element_type=jnp.float32)
    rotated = rotated + jnp.dot(across, rows_for(position ^ 2), preferred_element_type=jnp.float32)
    rotated = rotated + jnp.dot(
        diagonal, rows_for(position ^ 3), preferred_element_type=jnp.float32
    )
    return rotated


def solution(mesh):
    return jax.shard_map(
        body,
        mesh=mesh,
        in_specs=(P("dom", "st"), P("dom"), P("dom"), P(), P("dom", None), P("dom"), P(None, "st")),
        out_specs=P("dom", "st"),
        check_vma=False,
    )
```

```python
import jax
import jax.numpy as jnp
from jax import lax
from jax.sharding import PartitionSpec as P

POLY = 3


centre = 10.0
half_span = 10.0


def ring(block, axis, step):
    count = lax.axis_size(axis)
    route = [(i, (i + step) % count) for i in range(count)]
    return lax.ppermute(block, axis, route)


def from_partner(block, axis, distance):
    count = lax.axis_size(axis)
    route = []
    for low in range(count):
        high = low | 1 << distance
        if high != low and high < count:
            route += [(low, high), (high, low)]
    return lax.ppermute(block, axis, route)


def high_low(value):
    high = lax.reduce_precision(value, exponent_bits=8, mantissa_bits=7)
    low = value - high
    return jnp.concatenate([high.astype(jnp.bfloat16), low.astype(jnp.bfloat16)], 1)


def summed_halves(both):
    width = both.shape[1] // 2
    return both[:, :width] + both[:, width:]


def body(states, inv_mass, potential, cell_matrix, connect, face_rows, rotation):
    node_count, state_count = states.shape
    cell_count, cell_size = connect.shape
    face_count = face_rows.shape[0]
    wide_count = node_count + face_count
    pad = (-cell_size) % 16
    padded_size = cell_size + pad
    cell_rows = jnp.pad(connect, ((0, 0), (0, pad)), constant_values=-1).reshape(-1)
    padded_matrix = jnp.pad(cell_matrix, ((0, pad), (0, pad)))
    wide_ids = lax.broadcasted_iota(jnp.int32, (wide_count, 1), 0)
    gather_sel = (cell_rows[:, None] == wide_ids[:, 0][None, :]).astype(jnp.bfloat16)
    scatter_sel = (wide_ids == cell_rows[None, :]).astype(jnp.bfloat16)
    rim_ids = jnp.concatenate([face_rows, wide_ids[node_count:, 0]], 0)
    rim_sel = (rim_ids[:, None] == cell_rows[None, :]).astype(jnp.bfloat16)
    face_put = (wide_ids[:node_count] == face_rows[None, :]).astype(jnp.bfloat16)
    face_take = (face_rows[:, None] == wide_ids[:node_count, 0][None, :]).astype(jnp.bfloat16)

    face_states = jnp.dot(face_take, states, preferred_element_type=jnp.float32)
    face_mass_potential = lax.dot_general(
        jnp.stack([inv_mass, potential], 0),
        face_put.astype(jnp.float32),
        (((1,), (0,)), ((), ())),
        precision=lax.Precision.HIGHEST,
        preferred_element_type=jnp.float32,
    )
    ghost_states, ghost_mass_potential = ring((face_states, face_mass_potential), "dom", -1)
    field_start = jnp.concatenate([states.astype(jnp.float32), ghost_states], 0)
    wide_mass = jnp.concatenate([inv_mass, ghost_mass_potential[0]], 0)
    wide_potential = jnp.concatenate([potential, ghost_mass_potential[1]], 0)

    def operate(field_in):
        weighted = (wide_mass[:, None] * field_in).astype(jnp.bfloat16)
        values = lax.dot_general(
            scatter_sel, weighted, (((0,), (0,)), ((), ())), preferred_element_type=jnp.float32
        )
        values = values.astype(jnp.bfloat16).reshape(cell_count, padded_size, state_count)
        products = jnp.einsum(
            "ij,cjb->cib", padded_matrix, values, preferred_element_type=jnp.float32
        ).reshape(-1, state_count)
        both = high_low(products)
        ghost_part = summed_halves(
            jnp.dot(rim_sel[face_count:], both, preferred_element_type=jnp.float32)
        )
        from_prev = ring(ghost_part, "dom", 1)
        ghost_part, both = lax.optimization_barrier((ghost_part, both))
        face_part = summed_halves(
            jnp.dot(rim_sel[:face_count], both, preferred_element_type=jnp.float32)
        )
        from_next = ring(face_part, "dom", -1)
        rim = jnp.concatenate([face_part, ghost_part], 0)
        main = summed_halves(jnp.dot(scatter_sel, both, preferred_element_type=jnp.float32))
        own = main[:node_count] + summed_halves(
            jnp.dot(face_put, high_low(from_prev), preferred_element_type=jnp.float32)
        )
        summed = jnp.concatenate([own, main[node_count:] + from_next], 0)
        return wide_mass[:, None] * summed + wide_potential[:, None] * field_in

    def chebyshev_step(step, carry):
        previous, current = carry
        scaled = (operate(current) - centre * current) / half_span
        first = step == 0
        gain = jnp.where(first, 1.0, 2.0).astype(jnp.float32)
        keep = jnp.where(first, 0.0, 1.0).astype(jnp.float32)
        return current, gain * scaled - keep * previous

    previous, current = lax.fori_loop(0, POLY, chebyshev_step, (field_start, field_start))
    filtered = current[:node_count].astype(jnp.bfloat16)
    position = lax.axis_index("st") % 4

    def rows_for(member):
        return lax.dynamic_slice_in_dim(rotation, member * state_count, state_count, 0)

    across = from_partner(filtered, "st", 1)
    beside = from_partner(filtered, "st", 0)
    diagonal = from_partner(across, "st", 0)
    rotated = jnp.dot(filtered, rows_for(position), preferred_element_type=jnp.float32)
    rotated = rotated + jnp.dot(beside, rows_for(position ^ 1), preferred_element_type=jnp.float32)
    rotated = rotated + jnp.dot(across, rows_for(position ^ 2), preferred_element_type=jnp.float32)
    rotated = rotated + jnp.dot(
        diagonal, rows_for(position ^ 3), preferred_element_type=jnp.float32
    )
    return rotated


def solution(mesh):
    return jax.shard_map(
        body,
        mesh=mesh,
        in_specs=(P("dom", "st"), P("dom"), P("dom"), P(), P("dom", None), P("dom"), P(None, "st")),
        out_specs=P("dom", "st"),
        check_vma=False,
    )
```

```python
import jax
import jax.numpy as jnp
from jax import lax
from jax.sharding import PartitionSpec as P

POLY = 3


centre = 10.0
half_span = 10.0


def ring(block, axis, step):
    count = lax.axis_size(axis)
    route = [(i, (i + step) % count) for i in range(count)]
    return lax.ppermute(block, axis, route)


def from_partner(block, axis, distance):
    count = lax.axis_size(axis)
    route = []
    for low in range(count):
        high = low | 1 << distance
        if high != low and high < count:
            route += [(low, high), (high, low)]
    return lax.ppermute(block, axis, route)


def high_low(value):
    high = lax.reduce_precision(value, exponent_bits=8, mantissa_bits=7)
    low = value - high
    return jnp.concatenate([high.astype(jnp.bfloat16), low.astype(jnp.bfloat16)], 1)


def summed_halves(both):
    width = both.shape[1] // 2
    return both[:, :width] + both[:, width:]


def body(states, inv_mass, potential, cell_matrix, connect, face_rows, rotation):
    node_count, state_count = states.shape
    cell_count, cell_size = connect.shape
    face_count = face_rows.shape[0]
    wide_count = node_count + face_count
    pad = (-cell_size) % 16
    padded_size = cell_size + pad
    cell_rows = jnp.pad(connect, ((0, 0), (0, pad)), constant_values=-1).reshape(-1)
    padded_matrix = jnp.pad(cell_matrix, ((0, pad), (0, pad)))
    wide_ids = lax.broadcasted_iota(jnp.int32, (wide_count, 1), 0)
    gather_sel = (cell_rows[:, None] == wide_ids[:, 0][None, :]).astype(jnp.bfloat16)
    scatter_sel = (wide_ids == cell_rows[None, :]).astype(jnp.bfloat16)
    rim_ids = jnp.concatenate([face_rows, wide_ids[node_count:, 0]], 0)
    rim_sel = (rim_ids[:, None] == cell_rows[None, :]).astype(jnp.bfloat16)
    face_put = (wide_ids[:node_count] == face_rows[None, :]).astype(jnp.bfloat16)
    face_take = (face_rows[:, None] == wide_ids[:node_count, 0][None, :]).astype(jnp.bfloat16)

    face_states = jnp.dot(face_take, states, preferred_element_type=jnp.float32)
    face_mass_potential = lax.dot_general(
        jnp.stack([inv_mass, potential], 0),
        face_put.astype(jnp.float32),
        (((1,), (0,)), ((), ())),
        precision=lax.Precision.HIGHEST,
        preferred_element_type=jnp.float32,
    )
    ghost_states, ghost_mass_potential = ring((face_states, face_mass_potential), "dom", -1)
    field_start = jnp.concatenate([states.astype(jnp.float32), ghost_states], 0)
    wide_mass = jnp.concatenate([inv_mass, ghost_mass_potential[0]], 0)
    wide_potential = jnp.concatenate([potential, ghost_mass_potential[1]], 0)

    def operate(field_in):
        weighted = (wide_mass[:, None] * field_in).astype(jnp.bfloat16)
        values = lax.dot_general(
            scatter_sel, weighted, (((0,), (0,)), ((), ())), preferred_element_type=jnp.float32
        )
        values = values.astype(jnp.bfloat16).reshape(cell_count, padded_size, state_count)
        products = jnp.einsum(
            "ij,cjb->cib", padded_matrix, values, preferred_element_type=jnp.float32
        ).reshape(-1, state_count)
        both = high_low(products)
        rim = jnp.dot(rim_sel, both, preferred_element_type=jnp.float32)
        from_prev = summed_halves(ring(rim[face_count:], "dom", 1))
        from_next = summed_halves(ring(rim[:face_count], "dom", -1))
        main = summed_halves(jnp.dot(scatter_sel, both, preferred_element_type=jnp.float32))
        own = main[:node_count] + summed_halves(
            jnp.dot(face_put, high_low(from_prev), preferred_element_type=jnp.float32)
        )
        summed = jnp.concatenate([own, main[node_count:] + from_next], 0)
        return wide_mass[:, None] * summed + wide_potential[:, None] * field_in

    def chebyshev_step(step, carry):
        previous, current = carry
        scaled = (operate(current) - centre * current) / half_span
        first = step == 0
        gain = jnp.where(first, 1.0, 2.0).astype(jnp.float32)
        keep = jnp.where(first, 0.0, 1.0).astype(jnp.float32)
        return current, gain * scaled - keep * previous

    previous, current = lax.fori_loop(0, POLY, chebyshev_step, (field_start, field_start))
    filtered = current[:node_count].astype(jnp.bfloat16)
    position = lax.axis_index("st") % 4

    def rows_for(member):
        return lax.dynamic_slice_in_dim(rotation, member * state_count, state_count, 0)

    across = from_partner(filtered, "st", 1)
    beside = from_partner(filtered, "st", 0)
    diagonal = from_partner(across, "st", 0)
    rotated = jnp.dot(filtered, rows_for(position), preferred_element_type=jnp.float32)
    rotated = rotated + jnp.dot(beside, rows_for(position ^ 1), preferred_element_type=jnp.float32)
    rotated = rotated + jnp.dot(across, rows_for(position ^ 2), preferred_element_type=jnp.float32)
    rotated = rotated + jnp.dot(
        diagonal, rows_for(position ^ 3), preferred_element_type=jnp.float32
    )
    return rotated


def solution(mesh):
    return jax.shard_map(
        body,
        mesh=mesh,
        in_specs=(P("dom", "st"), P("dom"), P("dom"), P(), P("dom", None), P("dom"), P(None, "st")),
        out_specs=P("dom", "st"),
        check_vma=False,
    )
```

```python
import jax
import jax.numpy as jnp
from jax import lax
from jax.sharding import PartitionSpec as P

POLY = 3


centre = 10.0
half_span = 10.0


def ring(block, axis, step):
    count = lax.axis_size(axis)
    route = [(i, (i + step) % count) for i in range(count)]
    return lax.ppermute(block, axis, route)


def from_partner(block, axis, distance):
    count = lax.axis_size(axis)
    route = []
    for low in range(count):
        high = low | 1 << distance
        if high != low and high < count:
            route += [(low, high), (high, low)]
    return lax.ppermute(block, axis, route)


def high_low(value):
    high = lax.reduce_precision(value, exponent_bits=8, mantissa_bits=7)
    low = value - high
    return jnp.concatenate([high.astype(jnp.bfloat16), low.astype(jnp.bfloat16)], 1)


def summed_halves(both):
    width = both.shape[1] // 2
    return both[:, :width] + both[:, width:]


def body(states, inv_mass, potential, cell_matrix, connect, face_rows, rotation):
    node_count, state_count = states.shape
    cell_count, cell_size = connect.shape
    face_count = face_rows.shape[0]
    wide_count = node_count + face_count
    pad = (-cell_size) % 16
    padded_size = cell_size + pad
    cell_rows = jnp.pad(connect, ((0, 0), (0, pad)), constant_values=-1).reshape(-1)
    padded_matrix = jnp.pad(cell_matrix, ((0, pad), (0, pad)))
    wide_ids = lax.broadcasted_iota(jnp.int32, (wide_count, 1), 0)
    gather_sel = (cell_rows[:, None] == wide_ids[:, 0][None, :]).astype(jnp.bfloat16)
    scatter_sel = (wide_ids == cell_rows[None, :]).astype(jnp.bfloat16)
    rim_ids = jnp.concatenate([face_rows, wide_ids[node_count:, 0]], 0)
    rim_sel = (rim_ids[:, None] == cell_rows[None, :]).astype(jnp.bfloat16)
    face_put = (wide_ids[:node_count] == face_rows[None, :]).astype(jnp.bfloat16)
    face_take = (face_rows[:, None] == wide_ids[:node_count, 0][None, :]).astype(jnp.bfloat16)

    face_states = jnp.dot(face_take, states, preferred_element_type=jnp.bfloat16)
    face_mass_potential = lax.dot_general(
        jnp.stack([inv_mass, potential], 0),
        face_put.astype(jnp.float32),
        (((1,), (0,)), ((), ())),
        precision=lax.Precision.HIGHEST,
        preferred_element_type=jnp.float32,
    )
    ghost_states, ghost_mass_potential = ring((face_states, face_mass_potential), "dom", -1)
    field_start = jnp.concatenate([states, ghost_states], 0).astype(jnp.float32)
    wide_mass = jnp.concatenate([inv_mass, ghost_mass_potential[0]], 0)
    wide_potential = jnp.concatenate([potential, ghost_mass_potential[1]], 0)

    def operate(field_in):
        weighted = (wide_mass[:, None] * field_in).astype(jnp.bfloat16)
        values = lax.dot_general(
            scatter_sel, weighted, (((0,), (0,)), ((), ())), preferred_element_type=jnp.float32
        )
        values = values.astype(jnp.bfloat16).reshape(cell_count, padded_size, state_count)
        products = jnp.einsum(
            "ij,cjb->cib", padded_matrix, values, preferred_element_type=jnp.float32
        ).reshape(-1, state_count)
        both = high_low(products)
        rim = summed_halves(jnp.dot(rim_sel, both, preferred_element_type=jnp.float32))
        from_prev = ring(rim[face_count:], "dom", 1)
        from_next = ring(rim[:face_count], "dom", -1)
        main = summed_halves(jnp.dot(scatter_sel, both, preferred_element_type=jnp.float32))
        own = main[:node_count] + summed_halves(
            jnp.dot(face_put, high_low(from_prev), preferred_element_type=jnp.float32)
        )
        summed = jnp.concatenate([own, main[node_count:] + from_next], 0)
        return wide_mass[:, None] * summed + wide_potential[:, None] * field_in

    def chebyshev_step(step, carry):
        previous, current = carry
        scaled = (operate(current) - centre * current) / half_span
        first = step == 0
        gain = jnp.where(first, 1.0, 2.0).astype(jnp.float32)
        keep = jnp.where(first, 0.0, 1.0).astype(jnp.float32)
        return current, gain * scaled - keep * previous

    previous, current = lax.fori_loop(0, POLY, chebyshev_step, (field_start, field_start))
    filtered = current[:node_count].astype(jnp.bfloat16)
    position = lax.axis_index("st") % 4

    def rows_for(member):
        return lax.dynamic_slice_in_dim(rotation, member * state_count, state_count, 0)

    across = from_partner(filtered, "st", 1)
    beside = from_partner(filtered, "st", 0)
    diagonal = from_partner(across, "st", 0)
    rotated = jnp.dot(filtered, rows_for(position), preferred_element_type=jnp.float32)
    rotated = rotated + jnp.dot(beside, rows_for(position ^ 1), preferred_element_type=jnp.float32)
    rotated = rotated + jnp.dot(across, rows_for(position ^ 2), preferred_element_type=jnp.float32)
    rotated = rotated + jnp.dot(
        diagonal, rows_for(position ^ 3), preferred_element_type=jnp.float32
    )
    return rotated


def solution(mesh):
    return jax.shard_map(
        body,
        mesh=mesh,
        in_specs=(P("dom", "st"), P("dom"), P("dom"), P(), P("dom", None), P("dom"), P(None, "st")),
        out_specs=P("dom", "st"),
        check_vma=False,
    )
```
